32 devices in a mesh: grp: 2 (over x), ctx: 8 (over z, y), ch: 2 (over core).
Axes of the slice: x: 2, y: 2, z: 4, core: 2. Of those that a mesh axis runs over, the one named last changes fastest.
Arguments:
- inputs: bfloat16 [4096, 4096], P(('grp', 'ctx'), 'ch'), parts along dimension 0, may hold values from -0.125 to 0.125
- out_grad: bfloat16 [4096, 4096], P(('grp', 'ctx'), 'ch'), parts along dimension 0, may hold values from -50 to 50
- w_in: float32 [33, 64], replicated, may hold values from -1 to 1
- b_in: float32 [64], replicated, may hold values from -1 to 1
- w_mid: float32 [64, 64], replicated, may hold values from -0.75 to 0.75
- act_freq: float32 [64], replicated, may hold values from 1 to 24
- w_out: float32 [64, 4096], P(None, 'ch'), may hold values from -1 to 1
- decay_rate: float32 [4096], P('ch'), may hold values from 0.000234375 to 0.034
Outputs:
- grad_inputs: bfloat16 [4096, 4096], P(('grp', 'ctx'), 'ch'), parts along dimension 0
- grad_filter: float32 [2048, 4096], P(('grp', 'ctx'), 'ch'), parts along dimension 0
The draws below stay inside these ranges and needn't reach their ends.
There are 2 independent parts, one for each index of `grp`. The reference program is written for one: setup_inputs(seed, part) draws one part's arguments, and reference() takes and returns one part's arrays. A program takes and returns all parts, laid end to end along the dimension named above; an argument that names none is the same for every part. Nothing has to cross between parts.
All inputs are finite; a program needn't handle non-finite values.
Results may differ from the reference program's by a relative error of at most 0.009.
Values may be sent and summed in bfloat16 or wider, within the bound.
No kernel may reach another device: no remote copies, remote signals or barrier semaphores. Data moves between devices by JAX's collectives and lax.ppermute only.
A program may use at most 128 MiB of HBM per device.

```python
import math
import jax
import jax.numpy as jnp
from jax import lax

D = 4096
ORDER = 64
LAG_BLOCKS = 4
TOK_DEV = 256
FEATS = 33
SEQ = 2048
LAGS = 1024


def channel_levels(channel_count):
    indices = jnp.arange(1, channel_count + 1, dtype=jnp.int32)
    spread = (indices * 2531 % 4096).astype(jnp.float32) / 4096.0
    return jnp.exp(-math.log(10.0) * spread)


def channel_rates(key):
    pick_key = jax.random.fold_in(key, 71)
    quick_key = jax.random.fold_in(key, 72)
    steady_key = jax.random.fold_in(key, 73)
    fast_tenths = 5
    chosen = jax.random.randint(pick_key, (D,), 0, 10) < fast_tenths
    quick_rates = jnp.exp(jax.random.uniform(quick_key, (D,), jnp.float32, math.log(1.0 / 50.0), math.log(1.0 / 30.0)))
    steady_rates = jnp.exp(jax.random.uniform(steady_key, (D,), jnp.float32, math.log(0.25 / LAGS), math.log(2.0 / LAGS)))
    return jnp.where(chosen, quick_rates, steady_rates).astype(jnp.float32)


def draw_decay_rate(key, part):
    return channel_rates(key)


def draw_w_out(key, part):
    rates = channel_rates(key)
    lag_sum = jnp.expm1(-2.0 * rates * LAGS) / jnp.expm1(-2.0 * rates)
    column_scale = channel_levels(D) / jnp.sqrt(0.5 * ORDER * lag_sum)
    sample_key = jax.random.fold_in(key, 74)
    sample = jnp.clip(jax.random.normal(sample_key, (ORDER, D), jnp.float32), -4.0, 4.0)
    return sample * column_scale[None, :]


def draw_out_grad(key, part):
    sample_key = jax.random.fold_in(key, 75)
    sample = jnp.clip(jax.random.normal(sample_key, (SEQ, D), jnp.float32), -5.0, 5.0)
    return (sample / channel_levels(D)[None, :]).astype(jnp.bfloat16)


def block_levels(rng, dims, shards, low, high):
    def one(axis_at, blocks):
        heights = jax.random.uniform(jax.random.fold_in(jax.random.fold_in(rng, 6), axis_at), (blocks,), jnp.float32, low / len(shards), high / len(shards))
        return jnp.repeat(jnp.exp(heights), dims[axis_at] // blocks).reshape((-1,) + (1,) * (len(dims) - axis_at - 1))

    loudness = one(*shards[0])
    for cut in shards[1:]:
        loudness = loudness * one(*cut)
    return loudness


def gaussian(stream_key, extent, width, most, split=(), kind=jnp.bfloat16):
    values = jax.random.normal(stream_key, extent, jnp.float32) * width
    if len(split) > 0:
        values = block_levels(stream_key, extent, split, -0.22, 0.18) * values
    return jnp.clip(values, min=-most, max=most).astype(kind)


def setup_inputs(seed: int = 0, part: int = 0) -> dict:
    key_of = jax.random.split(jax.random.key(seed), 9)
    own_keys = jax.random.split(jax.random.fold_in(key_of[8], part), 9)
    inputs = gaussian(own_keys[0], (SEQ, D), (1.0 / SEQ ** 0.5), 0.125, ((0, 8), (1, 2)))
    out_grad = draw_out_grad(jax.random.fold_in(jax.random.fold_in(key_of[8], part), 71), part)
    w_in = gaussian(key_of[2], (FEATS, ORDER), FEATS ** -0.5, 1.0, (), jnp.float32)
    b_in = jnp.clip(jax.random.uniform(key_of[3], (ORDER,), jnp.float32, -1.0, 1.0), -1.0, 1.0)
    w_mid = gaussian(key_of[4], (ORDER, ORDER), ORDER ** -0.5, 0.75, (), jnp.float32)
    act_freq = jnp.clip(jnp.exp(jax.random.uniform(key_of[5], (ORDER,), jnp.float32, math.log(1.0), math.log(24.0))), 1.0, 24.0)
    w_out = draw_w_out(jax.random.fold_in(key_of[8], 71), part)
    decay_rate = draw_decay_rate(jax.random.fold_in(key_of[8], 71), part)
    return dict(inputs=inputs, out_grad=out_grad, w_in=w_in, b_in=b_in, w_mid=w_mid, act_freq=act_freq, w_out=w_out, decay_rate=decay_rate)


def dft_tables(tok_rows):
    freq_ids = jnp.arange(tok_rows, dtype=jnp.int32)
    product = (freq_ids[:, None] * freq_ids[None, :]) % (2 * tok_rows)
    angles = jnp.float32(math.pi) * product.astype(jnp.float32) / tok_rows
    cosine = jnp.cos(angles)
    sine_table = jnp.sin(angles)
    parity = jnp.where(freq_ids % 2 == 0, 1.0, -1.0).astype(jnp.float32)
    dc_row = (freq_ids == 0)[:, None]
    weights = jnp.where(dc_row, 1.0, 2.0).astype(jnp.float32)
    fwd_re = cosine.astype(jnp.bfloat16)
    fwd_im = jnp.where(dc_row, parity[None, :], -sine_table).astype(jnp.bfloat16)
    inv_re = ((weights * cosine).T / (2 * tok_rows)).astype(jnp.bfloat16)
    inv_im = (jnp.where(dc_row, parity[None, :], -2.0 * sine_table).T / (2 * tok_rows)).astype(jnp.bfloat16)
    return fwd_re, fwd_im, inv_re, inv_im, parity, dc_row


def filter_taps(lag_ids, lag_total, w_in, b_in, w_mid, act_freq, w_out, decay_rate):
    band_count = (w_in.shape[0] - 1) // 2
    harmonic = jnp.arange(1, band_count + 1, dtype=jnp.int32)
    phases = (lag_ids[:, None] * harmonic[None, :]) % lag_total
    angles = 2.0 * math.pi * phases.astype(jnp.float32) / lag_total
    lag_pos = lag_ids.astype(jnp.float32)[:, None]
    features = jnp.concatenate([lag_pos / lag_total, jnp.cos(angles), jnp.sin(angles)], axis=1)
    first_act = jnp.sin(act_freq * (jnp.dot(features, w_in, precision=lax.Precision.HIGHEST, preferred_element_type=jnp.float32) + b_in))
    second_act = jnp.sin(act_freq * jnp.dot(first_act, w_mid, precision=lax.Precision.HIGHEST, preferred_element_type=jnp.float32))
    raw_taps = jnp.dot(second_act, w_out, precision=lax.Precision.HIGHEST, preferred_element_type=jnp.float32)
    return (raw_taps * jnp.exp(-decay_rate[None, :] * lag_pos)).astype(jnp.bfloat16)


def conj_product(left_re, left_im, right_re, right_im, dc_row):
    cross_term = left_im * right_im
    real_part = left_re * right_re + jnp.where(dc_row, 0.0, cross_term)
    imag_part = jnp.where(dc_row, cross_term, left_re * right_im - left_im * right_re)
    return real_part, imag_part


def batch_spectrum(fwd_re, fwd_im, slabs_in):
    widened = slabs_in.astype(jnp.float32)
    real_part = jnp.einsum('fs,ksc->kfc', fwd_re.astype(jnp.float32), widened, precision=lax.Precision.HIGHEST)
    imag_part = jnp.einsum('fs,ksc->kfc', fwd_im.astype(jnp.float32), widened, precision=lax.Precision.HIGHEST)
    real_part = lax.optimization_barrier(real_part.astype(jnp.bfloat16))
    imag_part = lax.optimization_barrier(imag_part.astype(jnp.bfloat16))
    return real_part.astype(jnp.float32), imag_part.astype(jnp.float32)


def reference(inputs, out_grad, w_in, b_in, w_mid, act_freq, w_out, decay_rate):
    tok_rows = TOK_DEV
    slab_count = SEQ // TOK_DEV
    blocks = LAG_BLOCKS
    fwd_re, fwd_im, inv_re, inv_im, parity, dc_row = dft_tables(tok_rows)
    inv_re32 = inv_re.astype(jnp.float32)
    inv_im32 = inv_im.astype(jnp.float32)
    parity_col = parity[:, None]
    filter_rows = filter_taps(jnp.arange(LAGS, dtype=jnp.int32), LAGS, w_in, b_in, w_mid, act_freq, w_out, decay_rate)
    chan_block = math.gcd(D, 512)
    groups = D // chan_block

    def arrange(whole, leading):
        return whole.reshape(leading, tok_rows, groups, chan_block).transpose(2, 0, 1, 3)

    def per_group(operands):
        in_slabs, grad_slabs, tap_slabs = operands
        grad_re, grad_im = batch_spectrum(fwd_re, fwd_im, grad_slabs)
        padding = jnp.zeros((blocks + 1, tok_rows, chan_block), jnp.float32)
        grad_re = jnp.concatenate([grad_re, padding], axis=0)
        grad_im = jnp.concatenate([grad_im, padding], axis=0)
        pair_re = grad_re[:-1] + parity_col * grad_re[1:]
        pair_im = grad_im[:-1] + parity_col * grad_im[1:]
        input_re, input_im = batch_spectrum(fwd_re, fwd_im, in_slabs)
        tap_re, tap_im = batch_spectrum(fwd_re, fwd_im, tap_slabs)
        sum_re = jnp.zeros((slab_count, tok_rows, chan_block), jnp.float32)
        sum_im = jnp.zeros((slab_count, tok_rows, chan_block), jnp.float32)
        grad_rows = []
        for lag_block in range(blocks):
            shifted_re = pair_re[lag_block:lag_block + slab_count]
            shifted_im = pair_im[lag_block:lag_block + slab_count]
            part_re, part_im = conj_product(tap_re[lag_block], tap_im[lag_block], shifted_re, shifted_im, dc_row)
            sum_re = sum_re + part_re
            sum_im = sum_im + part_im
            term_re, term_im = conj_product(input_re, input_im, shifted_re, shifted_im, dc_row)
            total_re = lax.optimization_barrier(term_re.astype(jnp.bfloat16)).astype(jnp.float32).sum(axis=0)
            total_im = lax.optimization_barrier(term_im.astype(jnp.bfloat16)).astype(jnp.float32).sum(axis=0)
            grad_rows.append(jnp.dot(inv_re32, total_re, precision=lax.Precision.HIGHEST, preferred_element_type=jnp.float32)
                             + jnp.dot(inv_im32, total_im, precision=lax.Precision.HIGHEST, preferred_element_type=jnp.float32))
        mix_re = lax.optimization_barrier(sum_re.astype(jnp.bfloat16)).astype(jnp.float32)
        mix_im = lax.optimization_barrier(sum_im.astype(jnp.bfloat16)).astype(jnp.float32)
        grad_in = jnp.einsum('sf,kfc->ksc', inv_re32, mix_re, precision=lax.Precision.HIGHEST) + jnp.einsum('sf,kfc->ksc', inv_im32, mix_im, precision=lax.Precision.HIGHEST)
        return grad_in.astype(jnp.bfloat16), jnp.stack(grad_rows, axis=0)

    grad_in, grad_taps = lax.map(per_group, (arrange(inputs, slab_count), arrange(out_grad, slab_count), arrange(filter_rows, blocks)))
    grad_inputs = grad_in.transpose(1, 2, 0, 3).reshape(SEQ, D)
    grad_filter = grad_taps.transpose(1, 2, 0, 3).reshape(LAGS, D)
    return grad_inputs, grad_filter
```

```python
import math

import jax
import jax.numpy as jnp
from jax import lax
from jax.sharding import PartitionSpec as P

LAG_BLOCKS = 4


def from_behind(value, axis, steps):
    count = lax.axis_size(axis)
    leading, last = (max(0, -steps), min(count, count - steps))
    return lax.ppermute(value, axis, [(source, source + steps) for source in range(leading, last)])


def dft_tables(tok_rows):
    freq_ids = jnp.arange(tok_rows, dtype=jnp.int32)
    product = freq_ids[:, None] * freq_ids[None, :] % (2 * tok_rows)
    angles = jnp.float32(math.pi) * product.astype(jnp.float32) / tok_rows
    cosine = jnp.cos(angles)
    sine_table = jnp.sin(angles)
    parity = jnp.where(freq_ids % 2 == 0, 1.0, -1.0).astype(jnp.float32)
    dc_row = (freq_ids == 0)[:, None]
    weights = jnp.where(dc_row, 1.0, 2.0).astype(jnp.float32)
    fwd_re = cosine.astype(jnp.bfloat16)
    fwd_im = jnp.where(dc_row, parity[None, :], -sine_table).astype(jnp.bfloat16)
    inv_re = ((weights * cosine).T / (2 * tok_rows)).astype(jnp.bfloat16)
    inv_im = (jnp.where(dc_row, parity[None, :], -2.0 * sine_table).T / (2 * tok_rows)).astype(
        jnp.bfloat16
    )
    return (fwd_re, fwd_im, inv_re, inv_im, parity, dc_row)


def filter_taps(lag_ids, lag_total, w_in, b_in, w_mid, act_freq, w_out, decay_rate):
    band_count = (w_in.shape[0] - 1) // 2
    harmonic = jnp.arange(1, band_count + 1, dtype=jnp.int32)
    phases = lag_ids[:, None] * harmonic[None, :] % lag_total
    angles = 2.0 * math.pi * phases.astype(jnp.float32) / lag_total
    lag_pos = lag_ids.astype(jnp.float32)[:, None]
    features = jnp.concatenate([lag_pos / lag_total, jnp.cos(angles), jnp.sin(angles)], axis=1)
    first_act = jnp.sin(
        act_freq
        * (
            jnp.dot(
                features, w_in, precision=lax.Precision.HIGHEST, preferred_element_type=jnp.float32
            )
            + b_in
        )
    )
    second_act = jnp.sin(
        act_freq
        * jnp.dot(
            first_act, w_mid, precision=lax.Precision.HIGHEST, preferred_element_type=jnp.float32
        )
    )
    raw_taps = jnp.dot(
        second_act, w_out, precision=lax.Precision.HIGHEST, preferred_element_type=jnp.float32
    )
    return (raw_taps * jnp.exp(-decay_rate[None, :] * lag_pos)).astype(jnp.bfloat16)


def conj_product(left_re, left_im, right_re, right_im, dc_row):
    cross_term = left_im * right_im
    real_part = left_re * right_re + jnp.where(dc_row, 0.0, cross_term)
    imag_part = jnp.where(dc_row, cross_term, left_re * right_im - left_im * right_re)
    return (real_part, imag_part)


def slab_spectrum(fwd_re, fwd_im, slab_data):
    real_part = jnp.dot(fwd_re, slab_data, preferred_element_type=jnp.float32).astype(jnp.bfloat16)
    imag_part = jnp.dot(fwd_im, slab_data, preferred_element_type=jnp.float32).astype(jnp.bfloat16)
    return (real_part, imag_part)


def on_device(inputs, out_grad, w_in, b_in, w_mid, act_freq, w_out, decay_rate):
    tok_rows, chan_width = out_grad.shape
    fwd_re, fwd_im, inv_re, inv_im, parity, dc_row = dft_tables(tok_rows)
    parity_col = parity[:, None]
    lag_total = LAG_BLOCKS * tok_rows
    later_grads = [out_grad] + [
        from_behind(out_grad, "ctx", -hop_count) for hop_count in range(1, LAG_BLOCKS + 1)
    ]
    all_lags = jnp.arange(lag_total, dtype=jnp.int32)
    filter_rows = filter_taps(all_lags, lag_total, w_in, b_in, w_mid, act_freq, w_out, decay_rate)
    spectra = [slab_spectrum(fwd_re, fwd_im, received) for received in later_grads]
    pair_list = []
    for lag_block in range(LAG_BLOCKS):
        near_re, near_im = spectra[lag_block]
        far_re, far_im = spectra[lag_block + 1]
        pair_list.append(
            (
                near_re.astype(jnp.float32) + parity_col * far_re.astype(jnp.float32),
                near_im.astype(jnp.float32) + parity_col * far_im.astype(jnp.float32),
            )
        )
    sum_re = jnp.zeros((tok_rows, chan_width), jnp.float32)
    sum_im = jnp.zeros((tok_rows, chan_width), jnp.float32)
    for lag_block in range(LAG_BLOCKS):
        tap_re, tap_im = slab_spectrum(
            fwd_re, fwd_im, filter_rows[lag_block * tok_rows : (lag_block + 1) * tok_rows]
        )
        part_re, part_im = conj_product(
            tap_re.astype(jnp.float32),
            tap_im.astype(jnp.float32),
            pair_list[lag_block][0],
            pair_list[lag_block][1],
            dc_row,
        )
        sum_re = sum_re + part_re
        sum_im = sum_im + part_im
    mix_re = sum_re.astype(jnp.bfloat16)
    mix_im = sum_im.astype(jnp.bfloat16)
    grad_inputs = (
        jnp.dot(inv_re, mix_re, preferred_element_type=jnp.float32)
        + jnp.dot(inv_im, mix_im, preferred_element_type=jnp.float32)
    ).astype(jnp.bfloat16)
    input_re, input_im = slab_spectrum(fwd_re, fwd_im, inputs)
    grad_rows = []
    for lag_block in range(LAG_BLOCKS):
        term_re, term_im = conj_product(
            input_re.astype(jnp.float32),
            input_im.astype(jnp.float32),
            pair_list[lag_block][0],
            pair_list[lag_block][1],
            dc_row,
        )
        grad_rows.append(
            jnp.dot(inv_re, term_re.astype(jnp.bfloat16), preferred_element_type=jnp.float32)
            + jnp.dot(inv_im, term_im.astype(jnp.bfloat16), preferred_element_type=jnp.float32)
        )
    grad_filter = lax.psum_scatter(
        jnp.concatenate(grad_rows, axis=0), "ctx", scatter_dimension=0, tiled=True
    )
    return (grad_inputs, grad_filter)


def solution(mesh):
    placed = (
        P(("grp", "ctx"), "ch"),
        P(("grp", "ctx"), "ch"),
        P(),
        P(),
        P(),
        P(),
        P(None, "ch"),
        P("ch"),
    )
    return jax.shard_map(
        on_device,
        mesh=mesh,
        in_specs=placed,
        out_specs=(P(("grp", "ctx"), "ch"), P(("grp", "ctx"), "ch")),
        check_vma=False,
    )
```

```python
import math

import jax
import jax.numpy as jnp
from jax import lax
from jax.sharding import PartitionSpec as P

LAG_BLOCKS = 4


def from_behind(value, axis, steps):
    count = lax.axis_size(axis)
    leading, last = (max(0, -steps), min(count, count - steps))
    return lax.ppermute(value, axis, [(source, source + steps) for source in range(leading, last)])


def dft_tables(tok_rows):
    freq_ids = jnp.arange(tok_rows, dtype=jnp.int32)
    product = freq_ids[:, None] * freq_ids[None, :] % (2 * tok_rows)
    angles = jnp.float32(math.pi) * product.astype(jnp.float32) / tok_rows
    cosine = jnp.cos(angles)
    sine_table = jnp.sin(angles)
    parity = jnp.where(freq_ids % 2 == 0, 1.0, -1.0).astype(jnp.float32)
    dc_row = (freq_ids == 0)[:, None]
    weights = jnp.where(dc_row, 1.0, 2.0).astype(jnp.float32)
    fwd_re = cosine.astype(jnp.bfloat16)
    fwd_im = jnp.where(dc_row, parity[None, :], -sine_table).astype(jnp.bfloat16)
    inv_re = ((weights * cosine).T / (2 * tok_rows)).astype(jnp.bfloat16)
    inv_im = (jnp.where(dc_row, parity[None, :], -2.0 * sine_table).T / (2 * tok_rows)).astype(
        jnp.bfloat16
    )
    return (fwd_re, fwd_im, inv_re, inv_im, parity, dc_row)


def filter_taps(lag_ids, lag_total, w_in, b_in, w_mid, act_freq, w_out, decay_rate):
    band_count = (w_in.shape[0] - 1) // 2
    harmonic = jnp.arange(1, band_count + 1, dtype=jnp.int32)
    phases = lag_ids[:, None] * harmonic[None, :] % lag_total
    angles = 2.0 * math.pi * phases.astype(jnp.float32) / lag_total
    lag_pos = lag_ids.astype(jnp.float32)[:, None]
    features = jnp.concatenate([lag_pos / lag_total, jnp.cos(angles), jnp.sin(angles)], axis=1)
    first_act = jnp.sin(
        act_freq
        * (
            jnp.dot(
                features, w_in, precision=lax.Precision.HIGHEST, preferred_element_type=jnp.float32
            )
            + b_in
        )
    )
    second_act = jnp.sin(
        act_freq
        * jnp.dot(
            first_act, w_mid, precision=lax.Precision.HIGHEST, preferred_element_type=jnp.float32
        )
    )
    raw_taps = jnp.dot(
        second_act, w_out, precision=lax.Precision.HIGHEST, preferred_element_type=jnp.float32
    )
    return (raw_taps * jnp.exp(-decay_rate[None, :] * lag_pos)).astype(jnp.bfloat16)


def conj_product(left_re, left_im, right_re, right_im, dc_row):
    cross_term = left_im * right_im
    real_part = left_re * right_re + jnp.where(dc_row, 0.0, cross_term)
    imag_part = jnp.where(dc_row, cross_term, left_re * right_im - left_im * right_re)
    return (real_part, imag_part)


def slab_spectrum(fwd_re, fwd_im, slab_data):
    real_part = jnp.dot(fwd_re, slab_data, preferred_element_type=jnp.float32).astype(jnp.bfloat16)
    imag_part = jnp.dot(fwd_im, slab_data, preferred_element_type=jnp.float32).astype(jnp.bfloat16)
    return (real_part, imag_part)


def on_device(inputs, out_grad, w_in, b_in, w_mid, act_freq, w_out, decay_rate):
    tok_rows, chan_width = out_grad.shape
    fwd_re, fwd_im, inv_re, inv_im, parity, dc_row = dft_tables(tok_rows)
    parity_col = parity[:, None]
    lag_total = LAG_BLOCKS * tok_rows
    later_grads = [out_grad] + [
        from_behind(out_grad, "ctx", -hop_count) for hop_count in range(1, LAG_BLOCKS + 1)
    ]
    all_lags = jnp.arange(lag_total, dtype=jnp.int32)
    filter_rows = filter_taps(all_lags, lag_total, w_in, b_in, w_mid, act_freq, w_out, decay_rate)
    spectra = [slab_spectrum(fwd_re, fwd_im, received) for received in later_grads]
    pair_list = []
    for lag_block in range(LAG_BLOCKS):
        near_re, near_im = spectra[lag_block]
        far_re, far_im = spectra[lag_block + 1]
        pair_list.append(
            (
                near_re.astype(jnp.float32) + parity_col * far_re.astype(jnp.float32),
                near_im.astype(jnp.float32) + parity_col * far_im.astype(jnp.float32),
            )
        )
    sum_re = jnp.zeros((tok_rows, chan_width), jnp.float32)
    sum_im = jnp.zeros((tok_rows, chan_width), jnp.float32)
    for lag_block in range(LAG_BLOCKS):
        tap_re, tap_im = slab_spectrum(
            fwd_re, fwd_im, filter_rows[lag_block * tok_rows : (lag_block + 1) * tok_rows]
        )
        part_re, part_im = conj_product(
            tap_re.astype(jnp.float32),
            tap_im.astype(jnp.float32),
            pair_list[lag_block][0],
            pair_list[lag_block][1],
            dc_row,
        )
        sum_re = sum_re + part_re
        sum_im = sum_im + part_im
    mix_re = sum_re.astype(jnp.bfloat16)
    mix_im = sum_im.astype(jnp.bfloat16)
    grad_inputs = (
        jnp.dot(inv_re, mix_re, preferred_element_type=jnp.float32)
        + jnp.dot(inv_im, mix_im, preferred_element_type=jnp.float32)
    ).astype(jnp.bfloat16)
    input_re, input_im = slab_spectrum(fwd_re, fwd_im, inputs)
    grad_rows = []
    for lag_block in range(LAG_BLOCKS):
        term_re, term_im = conj_product(
            input_re.astype(jnp.float32),
            input_im.astype(jnp.float32),
            pair_list[lag_block][0],
            pair_list[lag_block][1],
            dc_row,
        )
        grad_rows.append(
            jnp.dot(inv_re, term_re.astype(jnp.bfloat16), preferred_element_type=jnp.float32)
            + jnp.dot(inv_im, term_im.astype(jnp.bfloat16), preferred_element_type=jnp.float32)
        )
    grad_filter = lax.psum_scatter(
        jnp.concatenate(grad_rows, axis=0).astype(jnp.bfloat16),
        "ctx",
        scatter_dimension=0,
        tiled=True,
    ).astype(jnp.float32)
    return (grad_inputs, grad_filter)


def solution(mesh):
    placed = (
        P(("grp", "ctx"), "ch"),
        P(("grp", "ctx"), "ch"),
        P(),
        P(),
        P(),
        P(),
        P(None, "ch"),
        P("ch"),
    )
    return jax.shard_map(
        on_device,
        mesh=mesh,
        in_specs=placed,
        out_specs=(P(("grp", "ctx"), "ch"), P(("grp", "ctx"), "ch")),
        check_vma=False,
    )
```

```python
import math

import jax
import jax.numpy as jnp
from jax import lax
from jax.sharding import PartitionSpec as P

LAG_BLOCKS = 4


def from_behind(value, axis, steps):
    count = lax.axis_size(axis)
    leading, last = (max(0, -steps), min(count, count - steps))
    return lax.ppermute(value, axis, [(source, source + steps) for source in range(leading, last)])


def swap_pairs(value, axis):
    count = lax.axis_size(axis)
    return lax.ppermute(value, axis, [(source, source ^ 1) for source in range(count)])


def gather_later(block):
    side_zero = lax.axis_index("ctx") % 2 == 0
    two_on = from_behind(block, "ctx", -2)
    four_on = from_behind(two_on, "ctx", -2)
    partner_two_on = swap_pairs(two_on, "ctx")
    partner_pick = swap_pairs(jnp.where(side_zero, four_on, block), "ctx")
    one_on = jnp.where(side_zero, partner_pick, partner_two_on)
    three_on = jnp.where(side_zero, partner_two_on, partner_pick)
    return [block, one_on, two_on, three_on, four_on]


def dft_tables(tok_rows):
    freq_ids = jnp.arange(tok_rows, dtype=jnp.int32)
    product = freq_ids[:, None] * freq_ids[None, :] % (2 * tok_rows)
    angles = jnp.float32(math.pi) * product.astype(jnp.float32) / tok_rows
    cosine = jnp.cos(angles)
    sine_table = jnp.sin(angles)
    parity = jnp.where(freq_ids % 2 == 0, 1.0, -1.0).astype(jnp.float32)
    dc_row = (freq_ids == 0)[:, None]
    weights = jnp.where(dc_row, 1.0, 2.0).astype(jnp.float32)
    fwd_re = cosine.astype(jnp.bfloat16)
    fwd_im = jnp.where(dc_row, parity[None, :], -sine_table).astype(jnp.bfloat16)
    inv_re = ((weights * cosine).T / (2 * tok_rows)).astype(jnp.bfloat16)
    inv_im = (jnp.where(dc_row, parity[None, :], -2.0 * sine_table).T / (2 * tok_rows)).astype(
        jnp.bfloat16
    )
    return (fwd_re, fwd_im, inv_re, inv_im, parity, dc_row)


def filter_taps(lag_ids, lag_total, w_in, b_in, w_mid, act_freq, w_out, decay_rate):
    band_count = (w_in.shape[0] - 1) // 2
    harmonic = jnp.arange(1, band_count + 1, dtype=jnp.int32)
    phases = lag_ids[:, None] * harmonic[None, :] % lag_total
    angles = 2.0 * math.pi * phases.astype(jnp.float32) / lag_total
    lag_pos = lag_ids.astype(jnp.float32)[:, None]
    features = jnp.concatenate([lag_pos / lag_total, jnp.cos(angles), jnp.sin(angles)], axis=1)
    first_act = jnp.sin(
        act_freq
        * (
            jnp.dot(
                features, w_in, precision=lax.Precision.HIGHEST, preferred_element_type=jnp.float32
            )
            + b_in
        )
    )
    second_act = jnp.sin(
        act_freq
        * jnp.dot(
            first_act, w_mid, precision=lax.Precision.HIGHEST, preferred_element_type=jnp.float32
        )
    )
    raw_taps = jnp.dot(
        second_act, w_out, precision=lax.Precision.HIGHEST, preferred_element_type=jnp.float32
    )
    return (raw_taps * jnp.exp(-decay_rate[None, :] * lag_pos)).astype(jnp.bfloat16)


def conj_product(left_re, left_im, right_re, right_im, dc_row):
    cross_term = left_im * right_im
    real_part = left_re * right_re + jnp.where(dc_row, 0.0, cross_term)
    imag_part = jnp.where(dc_row, cross_term, left_re * right_im - left_im * right_re)
    return (real_part, imag_part)


def slab_spectrum(fwd_re, fwd_im, slab_data):
    real_part = jnp.dot(fwd_re, slab_data, preferred_element_type=jnp.float32).astype(jnp.bfloat16)
    imag_part = jnp.dot(fwd_im, slab_data, preferred_element_type=jnp.float32).astype(jnp.bfloat16)
    return (real_part, imag_part)


def on_device(inputs, out_grad, w_in, b_in, w_mid, act_freq, w_out, decay_rate):
    tok_rows, chan_width = out_grad.shape
    fwd_re, fwd_im, inv_re, inv_im, parity, dc_row = dft_tables(tok_rows)
    parity_col = parity[:, None]
    lag_total = LAG_BLOCKS * tok_rows
    later_grads = gather_later(out_grad)
    all_lags = jnp.arange(lag_total, dtype=jnp.int32)
    filter_rows = filter_taps(all_lags, lag_total, w_in, b_in, w_mid, act_freq, w_out, decay_rate)
    spectra = [slab_spectrum(fwd_re, fwd_im, received) for received in later_grads]
    pair_list = []
    for lag_block in range(LAG_BLOCKS):
        near_re, near_im = spectra[lag_block]
        far_re, far_im = spectra[lag_block + 1]
        pair_list.append(
            (
                near_re.astype(jnp.float32) + parity_col * far_re.astype(jnp.float32),
                near_im.astype(jnp.float32) + parity_col * far_im.astype(jnp.float32),
            )
        )
    sum_re = jnp.zeros((tok_rows, chan_width), jnp.float32)
    sum_im = jnp.zeros((tok_rows, chan_width), jnp.float32)
    for lag_block in range(LAG_BLOCKS):
        tap_re, tap_im = slab_spectrum(
            fwd_re, fwd_im, filter_rows[lag_block * tok_rows : (lag_block + 1) * tok_rows]
        )
        part_re, part_im = conj_product(
            tap_re.astype(jnp.float32),
            tap_im.astype(jnp.float32),
            pair_list[lag_block][0],
            pair_list[lag_block][1],
            dc_row,
        )
        sum_re = sum_re + part_re
        sum_im = sum_im + part_im
    mix_re = sum_re.astype(jnp.bfloat16)
    mix_im = sum_im.astype(jnp.bfloat16)
    grad_inputs = (
        jnp.dot(inv_re, mix_re, preferred_element_type=jnp.float32)
        + jnp.dot(inv_im, mix_im, preferred_element_type=jnp.float32)
    ).astype(jnp.bfloat16)
    input_re, input_im = slab_spectrum(fwd_re, fwd_im, inputs)
    grad_rows = []
    for lag_block in range(LAG_BLOCKS):
        term_re, term_im = conj_product(
            input_re.astype(jnp.float32),
            input_im.astype(jnp.float32),
            pair_list[lag_block][0],
            pair_list[lag_block][1],
            dc_row,
        )
        grad_rows.append(
            jnp.dot(inv_re, term_re.astype(jnp.bfloat16), preferred_element_type=jnp.float32)
            + jnp.dot(inv_im, term_im.astype(jnp.bfloat16), preferred_element_type=jnp.float32)
        )
    grad_filter = lax.psum_scatter(
        jnp.concatenate(grad_rows, axis=0).astype(jnp.bfloat16),
        "ctx",
        scatter_dimension=0,
        tiled=True,
    ).astype(jnp.float32)
    return (grad_inputs, grad_filter)


def solution(mesh):
    placed = (
        P(("grp", "ctx"), "ch"),
        P(("grp", "ctx"), "ch"),
        P(),
        P(),
        P(),
        P(),
        P(None, "ch"),
        P("ch"),
    )
    return jax.shard_map(
        on_device,
        mesh=mesh,
        in_specs=placed,
        out_specs=(P(("grp", "ctx"), "ch"), P(("grp", "ctx"), "ch")),
        check_vma=False,
    )
```

```python
import math

import jax
import jax.numpy as jnp
from jax import lax
from jax.sharding import PartitionSpec as P

LAG_BLOCKS = 4
CHUNKS = 2


def from_behind(value, axis, steps):
    count = lax.axis_size(axis)
    leading, last = (max(0, -steps), min(count, count - steps))
    return lax.ppermute(value, axis, [(source, source + steps) for source in range(leading, last)])


def swap_pairs(value, axis):
    count = lax.axis_size(axis)
    return lax.ppermute(value, axis, [(source, source ^ 1) for source in range(count)])


def gather_later(block):
    side_zero = lax.axis_index("ctx") % 2 == 0
    two_on = from_behind(block, "ctx", -2)
    four_on = from_behind(two_on, "ctx", -2)
    partner_two_on = swap_pairs(two_on, "ctx")
    partner_pick = swap_pairs(jnp.where(side_zero, four_on, block), "ctx")
    one_on = jnp.where(side_zero, partner_pick, partner_two_on)
    three_on = jnp.where(side_zero, partner_two_on, partner_pick)
    return [block, one_on, two_on, three_on, four_on]


def dft_tables(tok_rows):
    freq_ids = jnp.arange(tok_rows, dtype=jnp.int32)
    product = freq_ids[:, None] * freq_ids[None, :] % (2 * tok_rows)
    angles = jnp.float32(math.pi) * product.astype(jnp.float32) / tok_rows
    cosine = jnp.cos(angles)
    sine_table = jnp.sin(angles)
    parity = jnp.where(freq_ids % 2 == 0, 1.0, -1.0).astype(jnp.float32)
    dc_row = (freq_ids == 0)[:, None]
    weights = jnp.where(dc_row, 1.0, 2.0).astype(jnp.float32)
    fwd_re = cosine.astype(jnp.bfloat16)
    fwd_im = jnp.where(dc_row, parity[None, :], -sine_table).astype(jnp.bfloat16)
    inv_re = ((weights * cosine).T / (2 * tok_rows)).astype(jnp.bfloat16)
    inv_im = (jnp.where(dc_row, parity[None, :], -2.0 * sine_table).T / (2 * tok_rows)).astype(
        jnp.bfloat16
    )
    return (fwd_re, fwd_im, inv_re, inv_im, parity, dc_row)


def filter_taps(lag_ids, lag_total, w_in, b_in, w_mid, act_freq, w_out, decay_rate):
    band_count = (w_in.shape[0] - 1) // 2
    harmonic = jnp.arange(1, band_count + 1, dtype=jnp.int32)
    phases = lag_ids[:, None] * harmonic[None, :] % lag_total
    angles = 2.0 * math.pi * phases.astype(jnp.float32) / lag_total
    lag_pos = lag_ids.astype(jnp.float32)[:, None]
    features = jnp.concatenate([lag_pos / lag_total, jnp.cos(angles), jnp.sin(angles)], axis=1)
    first_act = jnp.sin(
        act_freq
        * (
            jnp.dot(
                features, w_in, precision=lax.Precision.HIGHEST, preferred_element_type=jnp.float32
            )
            + b_in
        )
    )
    second_act = jnp.sin(
        act_freq
        * jnp.dot(
            first_act, w_mid, precision=lax.Precision.HIGHEST, preferred_element_type=jnp.float32
        )
    )
    raw_taps = jnp.dot(
        second_act, w_out, precision=lax.Precision.HIGHEST, preferred_element_type=jnp.float32
    )
    return (raw_taps * jnp.exp(-decay_rate[None, :] * lag_pos)).astype(jnp.bfloat16)


def conj_product(left_re, left_im, right_re, right_im, dc_row):
    cross_term = left_im * right_im
    real_part = left_re * right_re + jnp.where(dc_row, 0.0, cross_term)
    imag_part = jnp.where(dc_row, cross_term, left_re * right_im - left_im * right_re)
    return (real_part, imag_part)


def slab_spectrum(fwd_re, fwd_im, slab_data):
    real_part = jnp.dot(fwd_re, slab_data, preferred_element_type=jnp.float32).astype(jnp.bfloat16)
    imag_part = jnp.dot(fwd_im, slab_data, preferred_element_type=jnp.float32).astype(jnp.bfloat16)
    return (real_part, imag_part)


def chunk_work(inputs, out_grad, filter_rows, tables):
    tok_rows, chan_width = out_grad.shape
    fwd_re, fwd_im, inv_re, inv_im, parity, dc_row = tables
    parity_col = parity[:, None]
    later_grads = gather_later(out_grad)
    spectra = [slab_spectrum(fwd_re, fwd_im, received) for received in later_grads]
    pair_list = []
    for lag_block in range(LAG_BLOCKS):
        near_re, near_im = spectra[lag_block]
        far_re, far_im = spectra[lag_block + 1]
        pair_list.append(
            (
                near_re.astype(jnp.float32) + parity_col * far_re.astype(jnp.float32),
                near_im.astype(jnp.float32) + parity_col * far_im.astype(jnp.float32),
            )
        )
    sum_re = jnp.zeros((tok_rows, chan_width), jnp.float32)
    sum_im = jnp.zeros((tok_rows, chan_width), jnp.float32)
    for lag_block in range(LAG_BLOCKS):
        tap_re, tap_im = slab_spectrum(
            fwd_re, fwd_im, filter_rows[lag_block * tok_rows : (lag_block + 1) * tok_rows]
        )
        part_re, part_im = conj_product(
            tap_re.astype(jnp.float32),
            tap_im.astype(jnp.float32),
            pair_list[lag_block][0],
            pair_list[lag_block][1],
            dc_row,
        )
        sum_re = sum_re + part_re
        sum_im = sum_im + part_im
    mix_re = sum_re.astype(jnp.bfloat16)
    mix_im = sum_im.astype(jnp.bfloat16)
    grad_inputs = (
        jnp.dot(inv_re, mix_re, preferred_element_type=jnp.float32)
        + jnp.dot(inv_im, mix_im, preferred_element_type=jnp.float32)
    ).astype(jnp.bfloat16)
    input_re, input_im = slab_spectrum(fwd_re, fwd_im, inputs)
    grad_rows = []
    for lag_block in range(LAG_BLOCKS):
        term_re, term_im = conj_product(
            input_re.astype(jnp.float32),
            input_im.astype(jnp.float32),
            pair_list[lag_block][0],
            pair_list[lag_block][1],
            dc_row,
        )
        grad_rows.append(
            jnp.dot(inv_re, term_re.astype(jnp.bfloat16), preferred_element_type=jnp.float32)
            + jnp.dot(inv_im, term_im.astype(jnp.bfloat16), preferred_element_type=jnp.float32)
        )
    grad_filter = lax.psum_scatter(
        jnp.concatenate(grad_rows, axis=0).astype(jnp.bfloat16),
        "ctx",
        scatter_dimension=0,
        tiled=True,
    ).astype(jnp.float32)
    return (grad_inputs, grad_filter)


def on_device(inputs, out_grad, w_in, b_in, w_mid, act_freq, w_out, decay_rate):
    tok_rows, chan_width = out_grad.shape
    tables = dft_tables(tok_rows)
    lag_total = LAG_BLOCKS * tok_rows
    all_lags = jnp.arange(lag_total, dtype=jnp.int32)
    filter_rows = filter_taps(all_lags, lag_total, w_in, b_in, w_mid, act_freq, w_out, decay_rate)
    chunks = CHUNKS if chan_width % (CHUNKS * 128) == 0 else 1
    width = chan_width // chunks
    results = [
        chunk_work(
            inputs[:, part * width : (part + 1) * width],
            out_grad[:, part * width : (part + 1) * width],
            filter_rows[:, part * width : (part + 1) * width],
            tables,
        )
        for part in range(chunks)
    ]
    return (
        jnp.concatenate([pieces[0] for pieces in results], axis=1),
        jnp.concatenate([pieces[1] for pieces in results], axis=1),
    )


def solution(mesh):
    placed = (
        P(("grp", "ctx"), "ch"),
        P(("grp", "ctx"), "ch"),
        P(),
        P(),
        P(),
        P(),
        P(None, "ch"),
        P("ch"),
    )
    return jax.shard_map(
        on_device,
        mesh=mesh,
        in_specs=placed,
        out_specs=(P(("grp", "ctx"), "ch"), P(("grp", "ctx"), "ch")),
        check_vma=False,
    )
```

```python
import math

import jax
import jax.numpy as jnp
from jax import lax
from jax.sharding import PartitionSpec as P

LAG_BLOCKS = 4


def from_behind(value, axis, steps):
    count = lax.axis_size(axis)
    leading, last = (max(0, -steps), min(count, count - steps))
    return lax.ppermute(value, axis, [(source, source + steps) for source in range(leading, last)])


def swap_pairs(value, axis, from_side):
    count = lax.axis_size(axis)
    return lax.ppermute(
        value, axis, [(source, source ^ 1) for source in range(from_side, count, 2)]
    )


def gather_later(block):
    side_zero = lax.axis_index("ctx") % 2 == 0
    two_on = from_behind(block, "ctx", -2)
    partner_own = swap_pairs(block, "ctx", 1)
    four_on = from_behind(two_on, "ctx", -2)
    partner_two_on = lax.ppermute(
        two_on, "ctx", [(source, source ^ 1) for source in range(lax.axis_size("ctx"))]
    )
    partner_four_on = swap_pairs(four_on, "ctx", 0)
    one_on = jnp.where(side_zero, partner_own, partner_two_on)
    three_on = jnp.where(side_zero, partner_two_on, partner_four_on)
    return [block, one_on, two_on, three_on, four_on]


def dft_tables(tok_rows):
    freq_ids = jnp.arange(tok_rows, dtype=jnp.int32)
    product = freq_ids[:, None] * freq_ids[None, :] % (2 * tok_rows)
    angles = jnp.float32(math.pi) * product.astype(jnp.float32) / tok_rows
    cosine = jnp.cos(angles)
    sine_table = jnp.sin(angles)
    parity = jnp.where(freq_ids % 2 == 0, 1.0, -1.0).astype(jnp.float32)
    dc_row = (freq_ids == 0)[:, None]
    weights = jnp.where(dc_row, 1.0, 2.0).astype(jnp.float32)
    fwd_re = cosine.astype(jnp.bfloat16)
    fwd_im = jnp.where(dc_row, parity[None, :], -sine_table).astype(jnp.bfloat16)
    inv_re = ((weights * cosine).T / (2 * tok_rows)).astype(jnp.bfloat16)
    inv_im = (jnp.where(dc_row, parity[None, :], -2.0 * sine_table).T / (2 * tok_rows)).astype(
        jnp.bfloat16
    )
    return (fwd_re, fwd_im, inv_re, inv_im, parity, dc_row)


def filter_taps(lag_ids, lag_total, w_in, b_in, w_mid, act_freq, w_out, decay_rate):
    band_count = (w_in.shape[0] - 1) // 2
    harmonic = jnp.arange(1, band_count + 1, dtype=jnp.int32)
    phases = lag_ids[:, None] * harmonic[None, :] % lag_total
    angles = 2.0 * math.pi * phases.astype(jnp.float32) / lag_total
    lag_pos = lag_ids.astype(jnp.float32)[:, None]
    features = jnp.concatenate([lag_pos / lag_total, jnp.cos(angles), jnp.sin(angles)], axis=1)
    first_act = jnp.sin(
        act_freq
        * (
            jnp.dot(
                features, w_in, precision=lax.Precision.HIGHEST, preferred_element_type=jnp.float32
            )
            + b_in
        )
    )
    second_act = jnp.sin(
        act_freq
        * jnp.dot(
            first_act, w_mid, precision=lax.Precision.HIGHEST, preferred_element_type=jnp.float32
        )
    )
    raw_taps = jnp.dot(
        second_act, w_out, precision=lax.Precision.HIGHEST, preferred_element_type=jnp.float32
    )
    return (raw_taps * jnp.exp(-decay_rate[None, :] * lag_pos)).astype(jnp.bfloat16)


def conj_product(left_re, left_im, right_re, right_im, dc_row):
    cross_term = left_im * right_im
    real_part = left_re * right_re + jnp.where(dc_row, 0.0, cross_term)
    imag_part = jnp.where(dc_row, cross_term, left_re * right_im - left_im * right_re)
    return (real_part, imag_part)


def slab_spectrum(fwd_re, fwd_im, slab_data):
    real_part = jnp.dot(fwd_re, slab_data, preferred_element_type=jnp.float32).astype(jnp.bfloat16)
    imag_part = jnp.dot(fwd_im, slab_data, preferred_element_type=jnp.float32).astype(jnp.bfloat16)
    return (real_part, imag_part)


def on_device(inputs, out_grad, w_in, b_in, w_mid, act_freq, w_out, decay_rate):
    tok_rows, chan_width = out_grad.shape
    fwd_re, fwd_im, inv_re, inv_im, parity, dc_row = dft_tables(tok_rows)
    parity_col = parity[:, None]
    lag_total = LAG_BLOCKS * tok_rows
    later_grads = gather_later(out_grad)
    all_lags = jnp.arange(lag_total, dtype=jnp.int32)
    filter_rows = filter_taps(all_lags, lag_total, w_in, b_in, w_mid, act_freq, w_out, decay_rate)
    spectra = [slab_spectrum(fwd_re, fwd_im, received) for received in later_grads]
    pair_list = []
    for lag_block in range(LAG_BLOCKS):
        near_re, near_im = spectra[lag_block]
        far_re, far_im = spectra[lag_block + 1]
        pair_list.append(
            (
                near_re.astype(jnp.float32) + parity_col * far_re.astype(jnp.float32),
                near_im.astype(jnp.float32) + parity_col * far_im.astype(jnp.float32),
            )
        )
    sum_re = jnp.zeros((tok_rows, chan_width), jnp.float32)
    sum_im = jnp.zeros((tok_rows, chan_width), jnp.float32)
    for lag_block in range(LAG_BLOCKS):
        tap_re, tap_im = slab_spectrum(
            fwd_re, fwd_im, filter_rows[lag_block * tok_rows : (lag_block + 1) * tok_rows]
        )
        part_re, part_im = conj_product(
            tap_re.astype(jnp.float32),
            tap_im.astype(jnp.float32),
            pair_list[lag_block][0],
            pair_list[lag_block][1],
            dc_row,
        )
        sum_re = sum_re + part_re
        sum_im = sum_im + part_im
    mix_re = sum_re.astype(jnp.bfloat16)
    mix_im = sum_im.astype(jnp.bfloat16)
    grad_inputs = (
        jnp.dot(inv_re, mix_re, preferred_element_type=jnp.float32)
        + jnp.dot(inv_im, mix_im, preferred_element_type=jnp.float32)
    ).astype(jnp.bfloat16)
    input_re, input_im = slab_spectrum(fwd_re, fwd_im, inputs)
    grad_rows = []
    for lag_block in range(LAG_BLOCKS):
        term_re, term_im = conj_product(
            input_re.astype(jnp.float32),
            input_im.astype(jnp.float32),
            pair_list[lag_block][0],
            pair_list[lag_block][1],
            dc_row,
        )
        grad_rows.append(
            jnp.dot(inv_re, term_re.astype(jnp.bfloat16), preferred_element_type=jnp.float32)
            + jnp.dot(inv_im, term_im.astype(jnp.bfloat16), preferred_element_type=jnp.float32)
        )
    grad_filter = lax.psum_scatter(
        jnp.concatenate(grad_rows, axis=0).astype(jnp.bfloat16),
        "ctx",
        scatter_dimension=0,
        tiled=True,
    ).astype(jnp.float32)
    return (grad_inputs, grad_filter)


def solution(mesh):
    placed = (
        P(("grp", "ctx"), "ch"),
        P(("grp", "ctx"), "ch"),
        P(),
        P(),
        P(),
        P(),
        P(None, "ch"),
        P("ch"),
    )
    return jax.shard_map(
        on_device,
        mesh=mesh,
        in_specs=placed,
        out_specs=(P(("grp", "ctx"), "ch"), P(("grp", "ctx"), "ch")),
        check_vma=False,
    )
```

```python
import math

import jax
import jax.numpy as jnp
from jax import lax
from jax.sharding import PartitionSpec as P

LAG_BLOCKS = 4


def from_behind(value, axis, steps):
    count = lax.axis_size(axis)
    leading, last = (max(0, -steps), min(count, count - steps))
    return lax.ppermute(value, axis, [(source, source + steps) for source in range(leading, last)])


def swap_pairs(value, axis, from_side):
    count = lax.axis_size(axis)
    return lax.ppermute(
        value, axis, [(source, source ^ 1) for source in range(from_side, count, 2)]
    )


def gather_later(block):
    side_zero = lax.axis_index("ctx") % 2 == 0
    two_on = from_behind(block, "ctx", -2)
    partner_own = swap_pairs(block, "ctx", 1)
    four_on = from_behind(two_on, "ctx", -2)
    partner_two_on = lax.ppermute(
        two_on, "ctx", [(source, source ^ 1) for source in range(lax.axis_size("ctx"))]
    )
    partner_four_on = swap_pairs(four_on, "ctx", 0)
    one_on = jnp.where(side_zero, partner_own, partner_two_on)
    three_on = jnp.where(side_zero, partner_two_on, partner_four_on)
    return [block, one_on, two_on, three_on, four_on]


def dft_tables(tok_rows):
    freq_ids = jnp.arange(tok_rows, dtype=jnp.int32)
    product = freq_ids[:, None] * freq_ids[None, :] % (2 * tok_rows)
    angles = jnp.float32(math.pi) * product.astype(jnp.float32) / tok_rows
    cosine = jnp.cos(angles)
    sine_table = jnp.sin(angles)
    parity = jnp.where(freq_ids % 2 == 0, 1.0, -1.0).astype(jnp.float32)
    dc_row = (freq_ids == 0)[:, None]
    weights = jnp.where(dc_row, 1.0, 2.0).astype(jnp.float32)
    fwd_re = cosine.astype(jnp.bfloat16)
    fwd_im = jnp.where(dc_row, parity[None, :], -sine_table).astype(jnp.bfloat16)
    inv_re = ((weights * cosine).T / (2 * tok_rows)).astype(jnp.bfloat16)
    inv_im = (jnp.where(dc_row, parity[None, :], -2.0 * sine_table).T / (2 * tok_rows)).astype(
        jnp.bfloat16
    )
    return (fwd_re, fwd_im, inv_re, inv_im, parity, dc_row)


def filter_taps(lag_ids, lag_total, w_in, b_in, w_mid, act_freq, w_out, decay_rate):
    band_count = (w_in.shape[0] - 1) // 2
    harmonic = jnp.arange(1, band_count + 1, dtype=jnp.int32)
    phases = lag_ids[:, None] * harmonic[None, :] % lag_total
    angles = 2.0 * math.pi * phases.astype(jnp.float32) / lag_total
    lag_pos = lag_ids.astype(jnp.float32)[:, None]
    features = jnp.concatenate([lag_pos / lag_total, jnp.cos(angles), jnp.sin(angles)], axis=1)
    first_act = jnp.sin(
        act_freq
        * (
            jnp.dot(
                features, w_in, precision=lax.Precision.HIGHEST, preferred_element_type=jnp.float32
            )
            + b_in
        )
    )
    second_act = jnp.sin(
        act_freq
        * jnp.dot(
            first_act, w_mid, precision=lax.Precision.HIGHEST, preferred_element_type=jnp.float32
        )
    )
    raw_taps = jnp.dot(
        second_act, w_out, precision=lax.Precision.HIGHEST, preferred_element_type=jnp.float32
    )
    return (raw_taps * jnp.exp(-decay_rate[None, :] * lag_pos)).astype(jnp.bfloat16)


def conj_product(left_re, left_im, right_re, right_im, dc_row):
    cross_term = left_im * right_im
    real_part = left_re * right_re + jnp.where(dc_row, 0.0, cross_term)
    imag_part = jnp.where(dc_row, cross_term, left_re * right_im - left_im * right_re)
    return (real_part, imag_part)


def slab_spectrum(fwd_re, fwd_im, slab_data):
    rows = fwd_re.shape[0]
    both = jnp.dot(
        jnp.concatenate([fwd_re, fwd_im], axis=0), slab_data, preferred_element_type=jnp.float32
    ).astype(jnp.bfloat16)
    return (both[:rows], both[rows:])


def batch_spectrum(fwd_re, fwd_im, slabs):
    rows = fwd_re.shape[0]
    both = jnp.einsum(
        "fs,jsc->jfc",
        jnp.concatenate([fwd_re, fwd_im], axis=0),
        slabs,
        preferred_element_type=jnp.float32,
    ).astype(jnp.bfloat16)
    return (both[:, :rows], both[:, rows:])


def on_device(inputs, out_grad, w_in, b_in, w_mid, act_freq, w_out, decay_rate):
    tok_rows, chan_width = out_grad.shape
    fwd_re, fwd_im, inv_re, inv_im, parity, dc_row = dft_tables(tok_rows)
    parity_col = parity[:, None]
    lag_total = LAG_BLOCKS * tok_rows
    later_grads = gather_later(out_grad)
    all_lags = jnp.arange(lag_total, dtype=jnp.int32)
    filter_rows = filter_taps(all_lags, lag_total, w_in, b_in, w_mid, act_freq, w_out, decay_rate)
    spectra = [slab_spectrum(fwd_re, fwd_im, received) for received in later_grads]
    pair_list = []
    for lag_block in range(LAG_BLOCKS):
        near_re, near_im = spectra[lag_block]
        far_re, far_im = spectra[lag_block + 1]
        pair_list.append(
            (
                near_re.astype(jnp.float32) + parity_col * far_re.astype(jnp.float32),
                near_im.astype(jnp.float32) + parity_col * far_im.astype(jnp.float32),
            )
        )
    sum_re = jnp.zeros((tok_rows, chan_width), jnp.float32)
    sum_im = jnp.zeros((tok_rows, chan_width), jnp.float32)
    taps_re, taps_im = batch_spectrum(
        fwd_re, fwd_im, filter_rows.reshape(LAG_BLOCKS, tok_rows, chan_width)
    )
    for lag_block in range(LAG_BLOCKS):
        tap_re, tap_im = taps_re[lag_block], taps_im[lag_block]
        part_re, part_im = conj_product(
            tap_re.astype(jnp.float32),
            tap_im.astype(jnp.float32),
            pair_list[lag_block][0],
            pair_list[lag_block][1],
            dc_row,
        )
        sum_re = sum_re + part_re
        sum_im = sum_im + part_im
    mix_re = sum_re.astype(jnp.bfloat16)
    mix_im = sum_im.astype(jnp.bfloat16)
    inv_both = jnp.concatenate([inv_re, inv_im], axis=1)
    grad_inputs = jnp.dot(
        inv_both, jnp.concatenate([mix_re, mix_im], axis=0), preferred_element_type=jnp.float32
    ).astype(jnp.bfloat16)
    input_re, input_im = slab_spectrum(fwd_re, fwd_im, inputs)
    grad_rows = []
    for lag_block in range(LAG_BLOCKS):
        term_re, term_im = conj_product(
            input_re.astype(jnp.float32),
            input_im.astype(jnp.float32),
            pair_list[lag_block][0],
            pair_list[lag_block][1],
            dc_row,
        )
        grad_rows.append(
            jnp.dot(
                inv_both,
                jnp.concatenate([term_re, term_im], axis=0).astype(jnp.bfloat16),
                preferred_element_type=jnp.float32,
            )
        )
    grad_filter = lax.psum_scatter(
        jnp.concatenate(grad_rows, axis=0).astype(jnp.bfloat16),
        "ctx",
        scatter_dimension=0,
        tiled=True,
    ).astype(jnp.float32)
    return (grad_inputs, grad_filter)


def solution(mesh):
    placed = (
        P(("grp", "ctx"), "ch"),
        P(("grp", "ctx"), "ch"),
        P(),
        P(),
        P(),
        P(),
        P(None, "ch"),
        P("ch"),
    )
    return jax.shard_map(
        on_device,
        mesh=mesh,
        in_specs=placed,
        out_specs=(P(("grp", "ctx"), "ch"), P(("grp", "ctx"), "ch")),
        check_vma=False,
    )
```

```python
import math

import jax
import jax.numpy as jnp
from jax import lax
from jax.sharding import PartitionSpec as P

LAG_BLOCKS = 4
SEQ_AXES = ("row", "side")


def from_behind(value, axis, steps):
    count = lax.axis_size(axis)
    leading, last = (max(0, -steps), min(count, count - steps))
    return lax.ppermute(value, axis, [(source, source + steps) for source in range(leading, last)])


def swap_pairs(value, axis, from_side):
    count = lax.axis_size(axis)
    return lax.ppermute(
        value, axis, [(source, source ^ 1) for source in range(from_side, count, 2)]
    )


def gather_later(block):
    side_zero = lax.axis_index(SEQ_AXES) % 2 == 0
    two_on = from_behind(block, SEQ_AXES, -2)
    partner_own = swap_pairs(block, SEQ_AXES, 1)
    four_on = from_behind(two_on, SEQ_AXES, -2)
    partner_two_on = lax.ppermute(
        two_on, SEQ_AXES, [(source, source ^ 1) for source in range(lax.axis_size(SEQ_AXES))]
    )
    partner_four_on = swap_pairs(four_on, SEQ_AXES, 0)
    one_on = jnp.where(side_zero, partner_own, partner_two_on)
    three_on = jnp.where(side_zero, partner_two_on, partner_four_on)
    return [block, one_on, two_on, three_on, four_on]


def dft_tables(tok_rows):
    freq_ids = jnp.arange(tok_rows, dtype=jnp.int32)
    product = freq_ids[:, None] * freq_ids[None, :] % (2 * tok_rows)
    angles = jnp.float32(math.pi) * product.astype(jnp.float32) / tok_rows
    cosine = jnp.cos(angles)
    sine_table = jnp.sin(angles)
    parity = jnp.where(freq_ids % 2 == 0, 1.0, -1.0).astype(jnp.float32)
    dc_row = (freq_ids == 0)[:, None]
    weights = jnp.where(dc_row, 1.0, 2.0).astype(jnp.float32)
    fwd_re = cosine.astype(jnp.bfloat16)
    fwd_im = jnp.where(dc_row, parity[None, :], -sine_table).astype(jnp.bfloat16)
    inv_re = ((weights * cosine).T / (2 * tok_rows)).astype(jnp.bfloat16)
    inv_im = (jnp.where(dc_row, parity[None, :], -2.0 * sine_table).T / (2 * tok_rows)).astype(
        jnp.bfloat16
    )
    return (fwd_re, fwd_im, inv_re, inv_im, parity, dc_row)


def filter_taps(lag_ids, lag_total, w_in, b_in, w_mid, act_freq, w_out, decay_rate):
    band_count = (w_in.shape[0] - 1) // 2
    harmonic = jnp.arange(1, band_count + 1, dtype=jnp.int32)
    phases = lag_ids[:, None] * harmonic[None, :] % lag_total
    angles = 2.0 * math.pi * phases.astype(jnp.float32) / lag_total
    lag_pos = lag_ids.astype(jnp.float32)[:, None]
    features = jnp.concatenate([lag_pos / lag_total, jnp.cos(angles), jnp.sin(angles)], axis=1)
    first_act = jnp.sin(
        act_freq
        * (
            jnp.dot(
                features, w_in, precision=lax.Precision.HIGHEST, preferred_element_type=jnp.float32
            )
            + b_in
        )
    )
    second_act = jnp.sin(
        act_freq
        * jnp.dot(
            first_act, w_mid, precision=lax.Precision.HIGHEST, preferred_element_type=jnp.float32
        )
    )
    raw_taps = jnp.dot(
        second_act, w_out, precision=lax.Precision.HIGHEST, preferred_element_type=jnp.float32
    )
    return (raw_taps * jnp.exp(-decay_rate[None, :] * lag_pos)).astype(jnp.bfloat16)


def conj_product(left_re, left_im, right_re, right_im, dc_row):
    cross_term = left_im * right_im
    real_part = left_re * right_re + jnp.where(dc_row, 0.0, cross_term)
    imag_part = jnp.where(dc_row, cross_term, left_re * right_im - left_im * right_re)
    return (real_part, imag_part)


def slab_spectrum(fwd_re, fwd_im, slab_data):
    rows = fwd_re.shape[0]
    both = jnp.dot(
        jnp.concatenate([fwd_re, fwd_im], axis=0), slab_data, preferred_element_type=jnp.float32
    ).astype(jnp.bfloat16)
    return (both[:rows], both[rows:])


def batch_spectrum(fwd_re, fwd_im, slabs):
    rows = fwd_re.shape[0]
    both = jnp.einsum(
        "fs,jsc->jfc",
        jnp.concatenate([fwd_re, fwd_im], axis=0),
        slabs,
        preferred_element_type=jnp.float32,
    ).astype(jnp.bfloat16)
    return (both[:, :rows], both[:, rows:])


def on_device(inputs, out_grad, w_in, b_in, w_mid, act_freq, w_out, decay_rate):
    tok_rows, chan_width = out_grad.shape
    fwd_re, fwd_im, inv_re, inv_im, parity, dc_row = dft_tables(tok_rows)
    parity_col = parity[:, None]
    lag_total = LAG_BLOCKS * tok_rows
    later_grads = gather_later(out_grad)
    all_lags = jnp.arange(lag_total, dtype=jnp.int32)
    filter_rows = filter_taps(all_lags, lag_total, w_in, b_in, w_mid, act_freq, w_out, decay_rate)
    spectra = [slab_spectrum(fwd_re, fwd_im, received) for received in later_grads]
    pair_list = []
    for lag_block in range(LAG_BLOCKS):
        near_re, near_im = spectra[lag_block]
        far_re, far_im = spectra[lag_block + 1]
        pair_list.append(
            (
                near_re.astype(jnp.float32) + parity_col * far_re.astype(jnp.float32),
                near_im.astype(jnp.float32) + parity_col * far_im.astype(jnp.float32),
            )
        )
    sum_re = jnp.zeros((tok_rows, chan_width), jnp.float32)
    sum_im = jnp.zeros((tok_rows, chan_width), jnp.float32)
    taps_re, taps_im = batch_spectrum(
        fwd_re, fwd_im, filter_rows.reshape(LAG_BLOCKS, tok_rows, chan_width)
    )
    for lag_block in range(LAG_BLOCKS):
        tap_re, tap_im = taps_re[lag_block], taps_im[lag_block]
        part_re, part_im = conj_product(
            tap_re.astype(jnp.float32),
            tap_im.astype(jnp.float32),
            pair_list[lag_block][0],
            pair_list[lag_block][1],
            dc_row,
        )
        sum_re = sum_re + part_re
        sum_im = sum_im + part_im
    mix_re = sum_re.astype(jnp.bfloat16)
    mix_im = sum_im.astype(jnp.bfloat16)
    inv_both = jnp.concatenate([inv_re, inv_im], axis=1)
    grad_inputs = jnp.dot(
        inv_both, jnp.concatenate([mix_re, mix_im], axis=0), preferred_element_type=jnp.float32
    ).astype(jnp.bfloat16)
    input_re, input_im = slab_spectrum(fwd_re, fwd_im, inputs)
    grad_rows = []
    for lag_block in range(LAG_BLOCKS):
        term_re, term_im = conj_product(
            input_re.astype(jnp.float32),
            input_im.astype(jnp.float32),
            pair_list[lag_block][0],
            pair_list[lag_block][1],
            dc_row,
        )
        grad_rows.append(
            jnp.dot(
                inv_both,
                jnp.concatenate([term_re, term_im], axis=0).astype(jnp.bfloat16),
                preferred_element_type=jnp.float32,
            )
        )
    row_count = lax.axis_size("row")
    partial = jnp.concatenate(grad_rows, axis=0).astype(jnp.bfloat16)
    share = partial.shape[0] // (row_count * 2)
    staged = partial.reshape(row_count, 2, share, chan_width).transpose(1, 0, 2, 3)
    by_side = lax.psum_scatter(staged, "side", scatter_dimension=0, tiled=True)
    by_row = lax.psum_scatter(by_side, "row", scatter_dimension=1, tiled=True)
    grad_filter = by_row.reshape(share, chan_width).astype(jnp.float32)
    return (grad_inputs, grad_filter)


def solution(mesh):
    groups, blocks, cores = mesh.devices.shape
    mesh = jax.sharding.Mesh(
        mesh.devices.reshape(groups, blocks // 2, 2, cores), ("grp", "row", "side", "ch")
    )
    placed = (
        P(("grp", "row", "side"), "ch"),
        P(("grp", "row", "side"), "ch"),
        P(),
        P(),
        P(),
        P(),
        P(None, "ch"),
        P("ch"),
    )
    return jax.shard_map(
        on_device,
        mesh=mesh,
        in_specs=placed,
        out_specs=(P(("grp", "row", "side"), "ch"), P(("grp", "row", "side"), "ch")),
        check_vma=False,
    )
```

```python
import math

import jax
import jax.numpy as jnp
from jax import lax
from jax.sharding import PartitionSpec as P

LAG_BLOCKS = 4
SEQ_AXES = ("row", "side")


def from_behind(value, axis, steps):
    count = lax.axis_size(axis)
    leading, last = (max(0, -steps), min(count, count - steps))
    return lax.ppermute(value, axis, [(source, source + steps) for source in range(leading, last)])


def swap_pairs(value, axis, from_side, stride=2):
    count = lax.axis_size(axis)
    return lax.ppermute(
        value, axis, [(source, source ^ 1) for source in range(from_side, count, stride)]
    )


def lag_rows_total(blocks):
    return sum(block.shape[0] for block in blocks)


def gather_later(block):
    side_zero = lax.axis_index(SEQ_AXES) % 2 == 0
    two_on = from_behind(block, SEQ_AXES, -2)
    partner_own = swap_pairs(block, SEQ_AXES, 1)
    four_on = from_behind(two_on, SEQ_AXES, -2)
    partner_two_on = lax.ppermute(
        two_on, SEQ_AXES, [(source, source ^ 1) for source in range(lax.axis_size(SEQ_AXES))]
    )
    partner_four_on = swap_pairs(four_on, SEQ_AXES, 0)
    one_on = jnp.where(side_zero, partner_own, partner_two_on)
    three_on = jnp.where(side_zero, partner_two_on, partner_four_on)
    return [block, one_on, two_on, three_on, four_on]


def dft_tables(tok_rows):
    freq_ids = jnp.arange(tok_rows, dtype=jnp.int32)
    product = freq_ids[:, None] * freq_ids[None, :] % (2 * tok_rows)
    angles = jnp.float32(math.pi) * product.astype(jnp.float32) / tok_rows
    cosine = jnp.cos(angles)
    sine_table = jnp.sin(angles)
    parity = jnp.where(freq_ids % 2 == 0, 1.0, -1.0).astype(jnp.float32)
    dc_row = (freq_ids == 0)[:, None]
    weights = jnp.where(dc_row, 1.0, 2.0).astype(jnp.float32)
    fwd_re = cosine.astype(jnp.bfloat16)
    fwd_im = jnp.where(dc_row, parity[None, :], -sine_table).astype(jnp.bfloat16)
    inv_re = ((weights * cosine).T / (2 * tok_rows)).astype(jnp.bfloat16)
    inv_im = (jnp.where(dc_row, parity[None, :], -2.0 * sine_table).T / (2 * tok_rows)).astype(
        jnp.bfloat16
    )
    return (fwd_re, fwd_im, inv_re, inv_im, parity, dc_row)


def filter_taps(lag_ids, lag_total, w_in, b_in, w_mid, act_freq, w_out, decay_rate):
    band_count = (w_in.shape[0] - 1) // 2
    harmonic = jnp.arange(1, band_count + 1, dtype=jnp.int32)
    phases = lag_ids[:, None] * harmonic[None, :] % lag_total
    angles = 2.0 * math.pi * phases.astype(jnp.float32) / lag_total
    lag_pos = lag_ids.astype(jnp.float32)[:, None]
    features = jnp.concatenate([lag_pos / lag_total, jnp.cos(angles), jnp.sin(angles)], axis=1)
    first_act = jnp.sin(
        act_freq
        * (
            jnp.dot(
                features, w_in, precision=lax.Precision.HIGHEST, preferred_element_type=jnp.float32
            )
            + b_in
        )
    )
    second_act = jnp.sin(
        act_freq
        * jnp.dot(
            first_act, w_mid, precision=lax.Precision.HIGHEST, preferred_element_type=jnp.float32
        )
    )
    raw_taps = jnp.dot(
        second_act, w_out, precision=lax.Precision.HIGHEST, preferred_element_type=jnp.float32
    )
    return (raw_taps * jnp.exp(-decay_rate[None, :] * lag_pos)).astype(jnp.bfloat16)


def conj_product(left_re, left_im, right_re, right_im, dc_row):
    cross_term = left_im * right_im
    real_part = left_re * right_re + jnp.where(dc_row, 0.0, cross_term)
    imag_part = jnp.where(dc_row, cross_term, left_re * right_im - left_im * right_re)
    return (real_part, imag_part)


def slab_spectrum(fwd_re, fwd_im, slab_data):
    rows = fwd_re.shape[0]
    both = jnp.dot(
        jnp.concatenate([fwd_re, fwd_im], axis=0), slab_data, preferred_element_type=jnp.float32
    ).astype(jnp.bfloat16)
    return (both[:rows], both[rows:])


def batch_spectrum(fwd_re, fwd_im, slabs):
    rows = fwd_re.shape[0]
    both = jnp.einsum(
        "fs,jsc->jfc",
        jnp.concatenate([fwd_re, fwd_im], axis=0),
        slabs,
        preferred_element_type=jnp.float32,
    ).astype(jnp.bfloat16)
    return (both[:, :rows], both[:, rows:])


def on_device(inputs, out_grad, w_in, b_in, w_mid, act_freq, w_out, decay_rate):
    tok_rows, chan_width = out_grad.shape
    fwd_re, fwd_im, inv_re, inv_im, parity, dc_row = dft_tables(tok_rows)
    parity_col = parity[:, None]
    lag_total = LAG_BLOCKS * tok_rows
    later_grads = gather_later(out_grad)
    all_lags = jnp.arange(lag_total, dtype=jnp.int32)
    filter_rows = filter_taps(all_lags, lag_total, w_in, b_in, w_mid, act_freq, w_out, decay_rate)
    spectra = [slab_spectrum(fwd_re, fwd_im, received) for received in later_grads]
    pair_list = []
    for lag_block in range(LAG_BLOCKS):
        near_re, near_im = spectra[lag_block]
        far_re, far_im = spectra[lag_block + 1]
        pair_list.append(
            (
                near_re.astype(jnp.float32) + parity_col * far_re.astype(jnp.float32),
                near_im.astype(jnp.float32) + parity_col * far_im.astype(jnp.float32),
            )
        )
    sum_re = jnp.zeros((tok_rows, chan_width), jnp.float32)
    sum_im = jnp.zeros((tok_rows, chan_width), jnp.float32)
    taps_re, taps_im = batch_spectrum(
        fwd_re, fwd_im, filter_rows.reshape(LAG_BLOCKS, tok_rows, chan_width)
    )
    for lag_block in range(LAG_BLOCKS):
        tap_re, tap_im = taps_re[lag_block], taps_im[lag_block]
        part_re, part_im = conj_product(
            tap_re.astype(jnp.float32),
            tap_im.astype(jnp.float32),
            pair_list[lag_block][0],
            pair_list[lag_block][1],
            dc_row,
        )
        sum_re = sum_re + part_re
        sum_im = sum_im + part_im
    mix_re = sum_re.astype(jnp.bfloat16)
    mix_im = sum_im.astype(jnp.bfloat16)
    inv_both = jnp.concatenate([inv_re, inv_im], axis=1)
    grad_inputs = jnp.dot(
        inv_both, jnp.concatenate([mix_re, mix_im], axis=0), preferred_element_type=jnp.float32
    ).astype(jnp.bfloat16)
    input_re, input_im = slab_spectrum(fwd_re, fwd_im, inputs)
    grad_rows = []
    for lag_block in range(LAG_BLOCKS):
        term_re, term_im = conj_product(
            input_re.astype(jnp.float32),
            input_im.astype(jnp.float32),
            pair_list[lag_block][0],
            pair_list[lag_block][1],
            dc_row,
        )
        grad_rows.append(
            jnp.dot(
                inv_both,
                jnp.concatenate([term_re, term_im], axis=0).astype(jnp.bfloat16),
                preferred_element_type=jnp.float32,
            )
        )
    row_count = lax.axis_size("row")
    share = lag_rows_total(grad_rows) // (row_count * 2)
    side_zero = lax.axis_index("side") == 0
    parts = 2 if row_count % 2 == 0 else 1
    reduced = []
    for part in range(parts):
        chosen = grad_rows[part * LAG_BLOCKS // parts : (part + 1) * LAG_BLOCKS // parts]
        staged = jnp.concatenate(chosen, axis=0).reshape(-1, 2, share, chan_width)
        mine = jnp.where(side_zero, staged[:, 0], staged[:, 1])
        theirs = jnp.where(side_zero, staged[:, 1], staged[:, 0]).astype(jnp.bfloat16)
        reduced.append(mine + swap_pairs(theirs, SEQ_AXES, 0, 1).astype(jnp.float32))
    by_row = lax.psum_scatter(
        jnp.concatenate(reduced, axis=0).astype(jnp.bfloat16), "row", scatter_dimension=0, tiled=True
    )
    grad_filter = by_row.reshape(share, chan_width).astype(jnp.float32)
    return (grad_inputs, grad_filter)


def solution(mesh):
    groups, blocks, cores = mesh.devices.shape
    mesh = jax.sharding.Mesh(
        mesh.devices.reshape(groups, blocks // 2, 2, cores), ("grp", "row", "side", "ch")
    )
    placed = (
        P(("grp", "row", "side"), "ch"),
        P(("grp", "row", "side"), "ch"),
        P(),
        P(),
        P(),
        P(),
        P(None, "ch"),
        P("ch"),
    )
    return jax.shard_map(
        on_device,
        mesh=mesh,
        in_specs=placed,
        out_specs=(P(("grp", "row", "side"), "ch"), P(("grp", "row", "side"), "ch")),
        check_vma=False,
    )
```

```python
import math

import jax
import jax.numpy as jnp
from jax import lax
from jax.sharding import PartitionSpec as P

LAG_BLOCKS = 4
SEQ_AXES = ("row", "side")


def from_behind(value, axis, steps):
    count = lax.axis_size(axis)
    leading, last = (max(0, -steps), min(count, count - steps))
    return lax.ppermute(value, axis, [(source, source + steps) for source in range(leading, last)])


def swap_pairs(value, axis, from_side, stride=2):
    count = lax.axis_size(axis)
    return lax.ppermute(
        value, axis, [(source, source ^ 1) for source in range(from_side, count, stride)]
    )


def lag_rows_total(blocks):
    return sum(block.shape[0] for block in blocks)


def gather_later(block):
    side_zero = lax.axis_index(SEQ_AXES) % 2 == 0
    two_on = from_behind(block, SEQ_AXES, -2)
    partner_own = swap_pairs(block, SEQ_AXES, 1)
    four_on = from_behind(two_on, SEQ_AXES, -2)
    partner_two_on = lax.ppermute(
        two_on, SEQ_AXES, [(source, source ^ 1) for source in range(lax.axis_size(SEQ_AXES))]
    )
    partner_four_on = lax.ppermute(
        partner_two_on,
        SEQ_AXES,
        [(source, source - 2) for source in range(3, lax.axis_size(SEQ_AXES), 2)],
    )
    one_on = jnp.where(side_zero, partner_own, partner_two_on)
    three_on = jnp.where(side_zero, partner_two_on, partner_four_on)
    return [block, one_on, two_on, three_on, four_on]


def dft_tables(tok_rows):
    freq_ids = jnp.arange(tok_rows, dtype=jnp.int32)
    product = freq_ids[:, None] * freq_ids[None, :] % (2 * tok_rows)
    angles = jnp.float32(math.pi) * product.astype(jnp.float32) / tok_rows
    cosine = jnp.cos(angles)
    sine_table = jnp.sin(angles)
    parity = jnp.where(freq_ids % 2 == 0, 1.0, -1.0).astype(jnp.float32)
    dc_row = (freq_ids == 0)[:, None]
    weights = jnp.where(dc_row, 1.0, 2.0).astype(jnp.float32)
    fwd_re = cosine.astype(jnp.bfloat16)
    fwd_im = jnp.where(dc_row, parity[None, :], -sine_table).astype(jnp.bfloat16)
    inv_re = ((weights * cosine).T / (2 * tok_rows)).astype(jnp.bfloat16)
    inv_im = (jnp.where(dc_row, parity[None, :], -2.0 * sine_table).T / (2 * tok_rows)).astype(
        jnp.bfloat16
    )
    return (fwd_re, fwd_im, inv_re, inv_im, parity, dc_row)


def filter_taps(lag_ids, lag_total, w_in, b_in, w_mid, act_freq, w_out, decay_rate):
    band_count = (w_in.shape[0] - 1) // 2
    harmonic = jnp.arange(1, band_count + 1, dtype=jnp.int32)
    phases = lag_ids[:, None] * harmonic[None, :] % lag_total
    angles = 2.0 * math.pi * phases.astype(jnp.float32) / lag_total
    lag_pos = lag_ids.astype(jnp.float32)[:, None]
    features = jnp.concatenate([lag_pos / lag_total, jnp.cos(angles), jnp.sin(angles)], axis=1)
    first_act = jnp.sin(
        act_freq
        * (
            jnp.dot(
                features, w_in, precision=lax.Precision.HIGHEST, preferred_element_type=jnp.float32
            )
            + b_in
        )
    )
    second_act = jnp.sin(
        act_freq
        * jnp.dot(
            first_act, w_mid, precision=lax.Precision.HIGHEST, preferred_element_type=jnp.float32
        )
    )
    raw_taps = jnp.dot(
        second_act, w_out, precision=lax.Precision.HIGHEST, preferred_element_type=jnp.float32
    )
    return (raw_taps * jnp.exp(-decay_rate[None, :] * lag_pos)).astype(jnp.bfloat16)


def conj_product(left_re, left_im, right_re, right_im, dc_row):
    cross_term = left_im * right_im
    real_part = left_re * right_re + jnp.where(dc_row, 0.0, cross_term)
    imag_part = jnp.where(dc_row, cross_term, left_re * right_im - left_im * right_re)
    return (real_part, imag_part)


def slab_spectrum(fwd_re, fwd_im, slab_data):
    rows = fwd_re.shape[0]
    both = jnp.dot(
        jnp.concatenate([fwd_re, fwd_im], axis=0), slab_data, preferred_element_type=jnp.float32
    ).astype(jnp.bfloat16)
    return (both[:rows], both[rows:])


def batch_spectrum(fwd_re, fwd_im, slabs):
    rows = fwd_re.shape[0]
    both = jnp.einsum(
        "fs,jsc->jfc",
        jnp.concatenate([fwd_re, fwd_im], axis=0),
        slabs,
        preferred_element_type=jnp.float32,
    ).astype(jnp.bfloat16)
    return (both[:, :rows], both[:, rows:])


def on_device(inputs, out_grad, w_in, b_in, w_mid, act_freq, w_out, decay_rate):
    tok_rows, chan_width = out_grad.shape
    fwd_re, fwd_im, inv_re, inv_im, parity, dc_row = dft_tables(tok_rows)
    parity_col = parity[:, None]
    lag_total = LAG_BLOCKS * tok_rows
    later_grads = gather_later(out_grad)
    all_lags = jnp.arange(lag_total, dtype=jnp.int32)
    filter_rows = filter_taps(all_lags, lag_total, w_in, b_in, w_mid, act_freq, w_out, decay_rate)
    spectra = [slab_spectrum(fwd_re, fwd_im, received) for received in later_grads]
    pair_list = []
    for lag_block in range(LAG_BLOCKS):
        near_re, near_im = spectra[lag_block]
        far_re, far_im = spectra[lag_block + 1]
        pair_list.append(
            (
                near_re.astype(jnp.float32) + parity_col * far_re.astype(jnp.float32),
                near_im.astype(jnp.float32) + parity_col * far_im.astype(jnp.float32),
            )
        )
    sum_re = jnp.zeros((tok_rows, chan_width), jnp.float32)
    sum_im = jnp.zeros((tok_rows, chan_width), jnp.float32)
    taps_re, taps_im = batch_spectrum(
        fwd_re, fwd_im, filter_rows.reshape(LAG_BLOCKS, tok_rows, chan_width)
    )
    for lag_block in range(LAG_BLOCKS):
        tap_re, tap_im = taps_re[lag_block], taps_im[lag_block]
        part_re, part_im = conj_product(
            tap_re.astype(jnp.float32),
            tap_im.astype(jnp.float32),
            pair_list[lag_block][0],
            pair_list[lag_block][1],
            dc_row,
        )
        sum_re = sum_re + part_re
        sum_im = sum_im + part_im
    mix_re = sum_re.astype(jnp.bfloat16)
    mix_im = sum_im.astype(jnp.bfloat16)
    inv_both = jnp.concatenate([inv_re, inv_im], axis=1)
    grad_inputs = jnp.dot(
        inv_both, jnp.concatenate([mix_re, mix_im], axis=0), preferred_element_type=jnp.float32
    ).astype(jnp.bfloat16)
    input_re, input_im = slab_spectrum(fwd_re, fwd_im, inputs)
    grad_rows = []
    for lag_block in range(LAG_BLOCKS):
        term_re, term_im = conj_product(
            input_re.astype(jnp.float32),
            input_im.astype(jnp.float32),
            pair_list[lag_block][0],
            pair_list[lag_block][1],
            dc_row,
        )
        grad_rows.append(
            jnp.dot(
                inv_both,
                jnp.concatenate([term_re, term_im], axis=0).astype(jnp.bfloat16),
                preferred_element_type=jnp.float32,
            )
        )
    row_count = lax.axis_size("row")
    share = lag_rows_total(grad_rows) // (row_count * 2)
    side_zero = lax.axis_index("side") == 0
    parts = 2 if row_count % 2 == 0 else 1
    reduced = []
    for part in range(parts):
        chosen = grad_rows[part * LAG_BLOCKS // parts : (part + 1) * LAG_BLOCKS // parts]
        staged = jnp.concatenate(chosen, axis=0).reshape(-1, 2, share, chan_width)
        mine = jnp.where(side_zero, staged[:, 0], staged[:, 1])
        theirs = jnp.where(side_zero, staged[:, 1], staged[:, 0]).astype(jnp.bfloat16)
        reduced.append(mine + swap_pairs(theirs, SEQ_AXES, 0, 1).astype(jnp.float32))
    by_row = lax.psum_scatter(
        jnp.concatenate(reduced, axis=0).astype(jnp.bfloat16), "row", scatter_dimension=0, tiled=True
    )
    grad_filter = by_row.reshape(share, chan_width).astype(jnp.float32)
    return (grad_inputs, grad_filter)


def solution(mesh):
    groups, blocks, cores = mesh.devices.shape
    mesh = jax.sharding.Mesh(
        mesh.devices.reshape(groups, blocks // 2, 2, cores), ("grp", "row", "side", "ch")
    )
    placed = (
        P(("grp", "row", "side"), "ch"),
        P(("grp", "row", "side"), "ch"),
        P(),
        P(),
        P(),
        P(),
        P(None, "ch"),
        P("ch"),
    )
    return jax.shard_map(
        on_device,
        mesh=mesh,
        in_specs=placed,
        out_specs=(P(("grp", "row", "side"), "ch"), P(("grp", "row", "side"), "ch")),
        check_vma=False,
    )
```

```python
import math

import jax
import jax.numpy as jnp
from jax import lax
from jax.sharding import PartitionSpec as P

LAG_BLOCKS = 4
SEQ_AXES = ("row", "side")


def from_behind(value, axis, steps):
    count = lax.axis_size(axis)
    leading, last = (max(0, -steps), min(count, count - steps))
    return lax.ppermute(value, axis, [(source, source + steps) for source in range(leading, last)])


def swap_pairs(value, axis, from_side, stride=2):
    count = lax.axis_size(axis)
    return lax.ppermute(
        value, axis, [(source, source ^ 1) for source in range(from_side, count, stride)]
    )


def lag_rows_total(blocks):
    return sum(block.shape[0] for block in blocks)


def gather_later(block):
    side_zero = lax.axis_index(SEQ_AXES) % 2 == 0
    two_on = from_behind(block, SEQ_AXES, -2)
    partner_own = swap_pairs(block, SEQ_AXES, 1)
    four_on = from_behind(two_on, SEQ_AXES, -2)
    partner_two_on = lax.ppermute(
        two_on, SEQ_AXES, [(source, source ^ 1) for source in range(lax.axis_size(SEQ_AXES))]
    )
    partner_four_on = lax.ppermute(
        partner_two_on,
        SEQ_AXES,
        [(source, source - 2) for source in range(3, lax.axis_size(SEQ_AXES), 2)],
    )
    one_on = jnp.where(side_zero, partner_own, partner_two_on)
    three_on = jnp.where(side_zero, partner_two_on, partner_four_on)
    return [block, one_on, two_on, three_on, four_on]


def dft_tables(tok_rows):
    freq_ids = jnp.arange(tok_rows, dtype=jnp.int32)
    product = freq_ids[:, None] * freq_ids[None, :] % (2 * tok_rows)
    angles = jnp.float32(math.pi) * product.astype(jnp.float32) / tok_rows
    cosine = jnp.cos(angles)
    sine_table = jnp.sin(angles)
    parity = jnp.where(freq_ids % 2 == 0, 1.0, -1.0).astype(jnp.float32)
    dc_row = (freq_ids == 0)[:, None]
    weights = jnp.where(dc_row, 1.0, 2.0).astype(jnp.float32)
    fwd_re = cosine.astype(jnp.bfloat16)
    fwd_im = jnp.where(dc_row, parity[None, :], -sine_table).astype(jnp.bfloat16)
    inv_re = ((weights * cosine).T / (2 * tok_rows)).astype(jnp.bfloat16)
    inv_im = (jnp.where(dc_row, parity[None, :], -2.0 * sine_table).T / (2 * tok_rows)).astype(
        jnp.bfloat16
    )
    return (fwd_re, fwd_im, inv_re, inv_im, parity, dc_row)


def filter_taps(lag_ids, lag_total, w_in, b_in, w_mid, act_freq, w_out, decay_rate):
    band_count = (w_in.shape[0] - 1) // 2
    harmonic = jnp.arange(1, band_count + 1, dtype=jnp.int32)
    phases = lag_ids[:, None] * harmonic[None, :] % lag_total
    angles = 2.0 * math.pi * phases.astype(jnp.float32) / lag_total
    lag_pos = lag_ids.astype(jnp.float32)[:, None]
    features = jnp.concatenate([lag_pos / lag_total, jnp.cos(angles), jnp.sin(angles)], axis=1)
    first_act = jnp.sin(
        act_freq
        * (
            jnp.dot(
                features, w_in, precision=lax.Precision.HIGHEST, preferred_element_type=jnp.float32
            )
            + b_in
        )
    )
    second_act = jnp.sin(
        act_freq
        * jnp.dot(
            first_act, w_mid, precision=lax.Precision.HIGHEST, preferred_element_type=jnp.float32
        )
    )
    raw_taps = jnp.dot(
        second_act, w_out, precision=lax.Precision.HIGHEST, preferred_element_type=jnp.float32
    )
    return (raw_taps * jnp.exp(-decay_rate[None, :] * lag_pos)).astype(jnp.bfloat16)


def conj_product(left_re, left_im, right_re, right_im, dc_row):
    cross_term = left_im * right_im
    real_part = left_re * right_re + jnp.where(dc_row, 0.0, cross_term)
    imag_part = jnp.where(dc_row, cross_term, left_re * right_im - left_im * right_re)
    return (real_part, imag_part)


def slab_spectrum(fwd_re, fwd_im, slab_data):
    rows = fwd_re.shape[0]
    both = jnp.dot(
        jnp.concatenate([fwd_re, fwd_im], axis=0), slab_data, preferred_element_type=jnp.float32
    ).astype(jnp.bfloat16)
    return (both[:rows], both[rows:])


def batch_spectrum(fwd_re, fwd_im, slabs):
    rows = fwd_re.shape[0]
    both = jnp.einsum(
        "fs,jsc->jfc",
        jnp.concatenate([fwd_re, fwd_im], axis=0),
        slabs,
        preferred_element_type=jnp.float32,
    ).astype(jnp.bfloat16)
    return (both[:, :rows], both[:, rows:])


def on_device(inputs, out_grad, w_in, b_in, w_mid, act_freq, w_out, decay_rate):
    tok_rows, chan_width = out_grad.shape
    fwd_re, fwd_im, inv_re, inv_im, parity, dc_row = dft_tables(tok_rows)
    parity_col = parity[:, None]
    lag_total = LAG_BLOCKS * tok_rows
    later_grads = gather_later(out_grad)
    all_lags = jnp.arange(lag_total, dtype=jnp.int32)
    filter_rows = filter_taps(all_lags, lag_total, w_in, b_in, w_mid, act_freq, w_out, decay_rate)
    spectra = [slab_spectrum(fwd_re, fwd_im, received) for received in later_grads]
    pair_list = []
    for lag_block in range(LAG_BLOCKS):
        near_re, near_im = spectra[lag_block]
        far_re, far_im = spectra[lag_block + 1]
        pair_list.append(
            (
                near_re.astype(jnp.float32) + parity_col * far_re.astype(jnp.float32),
                near_im.astype(jnp.float32) + parity_col * far_im.astype(jnp.float32),
            )
        )
    sum_re = jnp.zeros((tok_rows, chan_width), jnp.float32)
    sum_im = jnp.zeros((tok_rows, chan_width), jnp.float32)
    taps_re, taps_im = batch_spectrum(
        fwd_re, fwd_im, filter_rows.reshape(LAG_BLOCKS, tok_rows, chan_width)
    )
    for lag_block in range(LAG_BLOCKS):
        tap_re, tap_im = taps_re[lag_block], taps_im[lag_block]
        part_re, part_im = conj_product(
            tap_re.astype(jnp.float32),
            tap_im.astype(jnp.float32),
            pair_list[lag_block][0],
            pair_list[lag_block][1],
            dc_row,
        )
        sum_re = sum_re + part_re
        sum_im = sum_im + part_im
    mix_re = sum_re.astype(jnp.bfloat16)
    mix_im = sum_im.astype(jnp.bfloat16)
    inv_both = jnp.concatenate([inv_re, inv_im], axis=1)
    grad_inputs = jnp.dot(
        inv_both, jnp.concatenate([mix_re, mix_im], axis=0), preferred_element_type=jnp.float32
    ).astype(jnp.bfloat16)
    input_re, input_im = slab_spectrum(fwd_re, fwd_im, inputs)
    grad_rows = []
    for lag_block in range(LAG_BLOCKS):
        term_re, term_im = conj_product(
            input_re.astype(jnp.float32),
            input_im.astype(jnp.float32),
            pair_list[lag_block][0],
            pair_list[lag_block][1],
            dc_row,
        )
        grad_rows.append(
            jnp.dot(
                inv_both,
                jnp.concatenate([term_re, term_im], axis=0).astype(jnp.bfloat16),
                preferred_element_type=jnp.float32,
            )
        )
    row_count = lax.axis_size("row")
    share = lag_rows_total(grad_rows) // (row_count * 2)
    side_zero = lax.axis_index("side") == 0
    bounds = [0, 1, 2, LAG_BLOCKS] if row_count % 4 == 0 else [0, LAG_BLOCKS]
    reduced = []
    for low, high in zip(bounds[:-1], bounds[1:]):
        chosen = grad_rows[low:high]
        staged = jnp.concatenate(chosen, axis=0).reshape(-1, 2, share, chan_width)
        mine = jnp.where(side_zero, staged[:, 0], staged[:, 1])
        theirs = jnp.where(side_zero, staged[:, 1], staged[:, 0]).astype(jnp.bfloat16)
        reduced.append(mine + swap_pairs(theirs, SEQ_AXES, 0, 1).astype(jnp.float32))
    by_row = lax.psum_scatter(
        jnp.concatenate(reduced, axis=0).astype(jnp.bfloat16), "row", scatter_dimension=0, tiled=True
    )
    grad_filter = by_row.reshape(share, chan_width).astype(jnp.float32)
    return (grad_inputs, grad_filter)


def solution(mesh):
    groups, blocks, cores = mesh.devices.shape
    mesh = jax.sharding.Mesh(
        mesh.devices.reshape(groups, blocks // 2, 2, cores), ("grp", "row", "side", "ch")
    )
    placed = (
        P(("grp", "row", "side"), "ch"),
        P(("grp", "row", "side"), "ch"),
        P(),
        P(),
        P(),
        P(),
        P(None, "ch"),
        P("ch"),
    )
    return jax.shard_map(
        on_device,
        mesh=mesh,
        in_specs=placed,
        out_specs=(P(("grp", "row", "side"), "ch"), P(("grp", "row", "side"), "ch")),
        check_vma=False,
    )
```

```python
import math

import jax
import jax.numpy as jnp
from jax import lax
from jax.sharding import PartitionSpec as P

LAG_BLOCKS = 4
SEQ_AXES = ("row", "side")


def from_behind(value, axis, steps):
    count = lax.axis_size(axis)
    leading, last = (max(0, -steps), min(count, count - steps))
    return lax.ppermute(value, axis, [(source, source + steps) for source in range(leading, last)])


def swap_pairs(value, axis, from_side, stride=2):
    count = lax.axis_size(axis)
    return lax.ppermute(
        value, axis, [(source, source ^ 1) for source in range(from_side, count, stride)]
    )


def lag_rows_total(blocks):
    return sum(block.shape[0] for block in blocks)


def gather_later(block):
    side_zero = lax.axis_index(SEQ_AXES) % 2 == 0
    width = block.shape[1]
    split = width // 2 if width % 256 == 0 else width
    first_two_on = from_behind(block[:, :split], SEQ_AXES, -2)
    first_two_on, rest = lax.optimization_barrier((first_two_on, block[:, split:]))
    two_on = jnp.concatenate([first_two_on, from_behind(rest, SEQ_AXES, -2)], axis=1)
    partner_own = swap_pairs(block, SEQ_AXES, 1)
    four_on = from_behind(two_on, SEQ_AXES, -2)
    partner_two_on = jnp.concatenate(
        [swap_pairs(first_two_on, SEQ_AXES, 0, 1), swap_pairs(two_on[:, split:], SEQ_AXES, 0, 1)],
        axis=1,
    )
    partner_four_on = lax.ppermute(
        partner_two_on,
        SEQ_AXES,
        [(source, source - 2) for source in range(3, lax.axis_size(SEQ_AXES), 2)],
    )
    one_on = jnp.where(side_zero, partner_own, partner_two_on)
    three_on = jnp.where(side_zero, partner_two_on, partner_four_on)
    return [block, one_on, two_on, three_on, four_on]


def dft_tables(tok_rows):
    freq_ids = jnp.arange(tok_rows, dtype=jnp.int32)
    product = freq_ids[:, None] * freq_ids[None, :] % (2 * tok_rows)
    angles = jnp.float32(math.pi) * product.astype(jnp.float32) / tok_rows
    cosine = jnp.cos(angles)
    sine_table = jnp.sin(angles)
    parity = jnp.where(freq_ids % 2 == 0, 1.0, -1.0).astype(jnp.float32)
    dc_row = (freq_ids == 0)[:, None]
    weights = jnp.where(dc_row, 1.0, 2.0).astype(jnp.float32)
    fwd_re = cosine.astype(jnp.bfloat16)
    fwd_im = jnp.where(dc_row, parity[None, :], -sine_table).astype(jnp.bfloat16)
    inv_re = ((weights * cosine).T / (2 * tok_rows)).astype(jnp.bfloat16)
    inv_im = (jnp.where(dc_row, parity[None, :], -2.0 * sine_table).T / (2 * tok_rows)).astype(
        jnp.bfloat16
    )
    return (fwd_re, fwd_im, inv_re, inv_im, parity, dc_row)


def filter_taps(lag_ids, lag_total, w_in, b_in, w_mid, act_freq, w_out, decay_rate):
    band_count = (w_in.shape[0] - 1) // 2
    harmonic = jnp.arange(1, band_count + 1, dtype=jnp.int32)
    phases = lag_ids[:, None] * harmonic[None, :] % lag_total
    angles = 2.0 * math.pi * phases.astype(jnp.float32) / lag_total
    lag_pos = lag_ids.astype(jnp.float32)[:, None]
    features = jnp.concatenate([lag_pos / lag_total, jnp.cos(angles), jnp.sin(angles)], axis=1)
    first_act = jnp.sin(
        act_freq
        * (
            jnp.dot(
                features, w_in, precision=lax.Precision.HIGHEST, preferred_element_type=jnp.float32
            )
            + b_in
        )
    )
    second_act = jnp.sin(
        act_freq
        * jnp.dot(
            first_act, w_mid, precision=lax.Precision.HIGHEST, preferred_element_type=jnp.float32
        )
    )
    raw_taps = jnp.dot(
        second_act, w_out, precision=lax.Precision.HIGHEST, preferred_element_type=jnp.float32
    )
    return (raw_taps * jnp.exp(-decay_rate[None, :] * lag_pos)).astype(jnp.bfloat16)


def conj_product(left_re, left_im, right_re, right_im, dc_row):
    cross_term = left_im * right_im
    real_part = left_re * right_re + jnp.where(dc_row, 0.0, cross_term)
    imag_part = jnp.where(dc_row, cross_term, left_re * right_im - left_im * right_re)
    return (real_part, imag_part)


def slab_spectrum(fwd_re, fwd_im, slab_data):
    rows = fwd_re.shape[0]
    both = jnp.dot(
        jnp.concatenate([fwd_re, fwd_im], axis=0), slab_data, preferred_element_type=jnp.float32
    ).astype(jnp.bfloat16)
    return (both[:rows], both[rows:])


def batch_spectrum(fwd_re, fwd_im, slabs):
    rows = fwd_re.shape[0]
    both = jnp.einsum(
        "fs,jsc->jfc",
        jnp.concatenate([fwd_re, fwd_im], axis=0),
        slabs,
        preferred_element_type=jnp.float32,
    ).astype(jnp.bfloat16)
    return (both[:, :rows], both[:, rows:])


def on_device(inputs, out_grad, w_in, b_in, w_mid, act_freq, w_out, decay_rate):
    tok_rows, chan_width = out_grad.shape
    fwd_re, fwd_im, inv_re, inv_im, parity, dc_row = dft_tables(tok_rows)
    parity_col = parity[:, None]
    lag_total = LAG_BLOCKS * tok_rows
    later_grads = gather_later(out_grad)
    all_lags = jnp.arange(lag_total, dtype=jnp.int32)
    filter_rows = filter_taps(all_lags, lag_total, w_in, b_in, w_mid, act_freq, w_out, decay_rate)
    spectra = [slab_spectrum(fwd_re, fwd_im, received) for received in later_grads]
    pair_list = []
    for lag_block in range(LAG_BLOCKS):
        near_re, near_im = spectra[lag_block]
        far_re, far_im = spectra[lag_block + 1]
        pair_list.append(
            (
                near_re.astype(jnp.float32) + parity_col * far_re.astype(jnp.float32),
                near_im.astype(jnp.float32) + parity_col * far_im.astype(jnp.float32),
            )
        )
    sum_re = jnp.zeros((tok_rows, chan_width), jnp.float32)
    sum_im = jnp.zeros((tok_rows, chan_width), jnp.float32)
    taps_re, taps_im = batch_spectrum(
        fwd_re, fwd_im, filter_rows.reshape(LAG_BLOCKS, tok_rows, chan_width)
    )
    for lag_block in range(LAG_BLOCKS):
        tap_re, tap_im = taps_re[lag_block], taps_im[lag_block]
        part_re, part_im = conj_product(
            tap_re.astype(jnp.float32),
            tap_im.astype(jnp.float32),
            pair_list[lag_block][0],
            pair_list[lag_block][1],
            dc_row,
        )
        sum_re = sum_re + part_re
        sum_im = sum_im + part_im
    mix_re = sum_re.astype(jnp.bfloat16)
    mix_im = sum_im.astype(jnp.bfloat16)
    inv_both = jnp.concatenate([inv_re, inv_im], axis=1)
    grad_inputs = jnp.dot(
        inv_both, jnp.concatenate([mix_re, mix_im], axis=0), preferred_element_type=jnp.float32
    ).astype(jnp.bfloat16)
    input_re, input_im = slab_spectrum(fwd_re, fwd_im, inputs)
    grad_rows = []
    for lag_block in range(LAG_BLOCKS):
        term_re, term_im = conj_product(
            input_re.astype(jnp.float32),
            input_im.astype(jnp.float32),
            pair_list[lag_block][0],
            pair_list[lag_block][1],
            dc_row,
        )
        grad_rows.append(
            jnp.dot(
                inv_both,
                jnp.concatenate([term_re, term_im], axis=0).astype(jnp.bfloat16),
                preferred_element_type=jnp.float32,
            )
        )
    row_count = lax.axis_size("row")
    share = lag_rows_total(grad_rows) // (row_count * 2)
    side_zero = lax.axis_index("side") == 0
    parts = 2 if row_count % 2 == 0 else 1
    reduced = []
    for part in range(parts):
        chosen = grad_rows[part * LAG_BLOCKS // parts : (part + 1) * LAG_BLOCKS // parts]
        staged = jnp.concatenate(chosen, axis=0).reshape(-1, 2, share, chan_width)
        mine = jnp.where(side_zero, staged[:, 0], staged[:, 1])
        theirs = jnp.where(side_zero, staged[:, 1], staged[:, 0]).astype(jnp.bfloat16)
        reduced.append(mine + swap_pairs(theirs, SEQ_AXES, 0, 1).astype(jnp.float32))
    by_row = lax.psum_scatter(
        jnp.concatenate(reduced, axis=0).astype(jnp.bfloat16), "row", scatter_dimension=0, tiled=True
    )
    grad_filter = by_row.reshape(share, chan_width).astype(jnp.float32)
    return (grad_inputs, grad_filter)


def solution(mesh):
    groups, blocks, cores = mesh.devices.shape
    mesh = jax.sharding.Mesh(
        mesh.devices.reshape(groups, blocks // 2, 2, cores), ("grp", "row", "side", "ch")
    )
    placed = (
        P(("grp", "row", "side"), "ch"),
        P(("grp", "row", "side"), "ch"),
        P(),
        P(),
        P(),
        P(),
        P(None, "ch"),
        P("ch"),
    )
    return jax.shard_map(
        on_device,
        mesh=mesh,
        in_specs=placed,
        out_specs=(P(("grp", "row", "side"), "ch"), P(("grp", "row", "side"), "ch")),
        check_vma=False,
    )
```

```python
import math

import jax
import jax.numpy as jnp
from jax import lax
from jax.sharding import PartitionSpec as P

LAG_BLOCKS = 4
SEQ_AXES = ("row", "side")


def from_behind(value, axis, steps):
    count = lax.axis_size(axis)
    leading, last = (max(0, -steps), min(count, count - steps))
    return lax.ppermute(value, axis, [(source, source + steps) for source in range(leading, last)])


def swap_pairs(value, axis, from_side, stride=2):
    count = lax.axis_size(axis)
    return lax.ppermute(
        value, axis, [(source, source ^ 1) for source in range(from_side, count, stride)]
    )


def lag_rows_total(blocks):
    return sum(block.shape[0] for block in blocks)


def gather_later(block):
    side_zero = lax.axis_index(SEQ_AXES) % 2 == 0
    width = block.shape[1]
    split = width // 2 if width % 256 == 0 else width
    first_two_on = from_behind(block[:, :split], SEQ_AXES, -2)
    first_two_on, rest = lax.optimization_barrier((first_two_on, block[:, split:]))
    two_on = jnp.concatenate([first_two_on, from_behind(rest, SEQ_AXES, -2)], axis=1)
    partner_own = swap_pairs(block, SEQ_AXES, 1)
    four_on = from_behind(two_on, SEQ_AXES, -2)
    partner_two_on = jnp.concatenate(
        [swap_pairs(first_two_on, SEQ_AXES, 0, 1), swap_pairs(two_on[:, split:], SEQ_AXES, 0, 1)],
        axis=1,
    )
    partner_four_on = lax.ppermute(
        partner_two_on,
        SEQ_AXES,
        [(source, source - 2) for source in range(3, lax.axis_size(SEQ_AXES), 2)],
    )
    one_on = jnp.where(side_zero, partner_own, partner_two_on)
    three_on = jnp.where(side_zero, partner_two_on, partner_four_on)
    return [block, one_on, two_on, three_on, four_on]


def dft_tables(tok_rows):
    freq_ids = jnp.arange(tok_rows, dtype=jnp.int32)
    product = freq_ids[:, None] * freq_ids[None, :] % (2 * tok_rows)
    angles = jnp.float32(math.pi) * product.astype(jnp.float32) / tok_rows
    cosine = jnp.cos(angles)
    sine_table = jnp.sin(angles)
    parity = jnp.where(freq_ids % 2 == 0, 1.0, -1.0).astype(jnp.float32)
    dc_row = (freq_ids == 0)[:, None]
    weights = jnp.where(dc_row, 1.0, 2.0).astype(jnp.float32)
    fwd_re = cosine.astype(jnp.bfloat16)
    fwd_im = jnp.where(dc_row, parity[None, :], -sine_table).astype(jnp.bfloat16)
    inv_re = ((weights * cosine).T / (2 * tok_rows)).astype(jnp.bfloat16)
    inv_im = (jnp.where(dc_row, parity[None, :], -2.0 * sine_table).T / (2 * tok_rows)).astype(
        jnp.bfloat16
    )
    return (fwd_re, fwd_im, inv_re, inv_im, parity, dc_row)


def filter_taps(lag_ids, lag_total, w_in, b_in, w_mid, act_freq, w_out, decay_rate):
    band_count = (w_in.shape[0] - 1) // 2
    harmonic = jnp.arange(1, band_count + 1, dtype=jnp.int32)
    phases = lag_ids[:, None] * harmonic[None, :] % lag_total
    angles = 2.0 * math.pi * phases.astype(jnp.float32) / lag_total
    lag_pos = lag_ids.astype(jnp.float32)[:, None]
    features = jnp.concatenate([lag_pos / lag_total, jnp.cos(angles), jnp.sin(angles)], axis=1)
    first_act = jnp.sin(
        act_freq
        * (
            jnp.dot(
                features, w_in, precision=lax.Precision.HIGHEST, preferred_element_type=jnp.float32
            )
            + b_in
        )
    )
    second_act = jnp.sin(
        act_freq
        * jnp.dot(
            first_act, w_mid, precision=lax.Precision.HIGHEST, preferred_element_type=jnp.float32
        )
    )
    raw_taps = jnp.dot(
        second_act, w_out, precision=lax.Precision.HIGHEST, preferred_element_type=jnp.float32
    )
    return (raw_taps * jnp.exp(-decay_rate[None, :] * lag_pos)).astype(jnp.bfloat16)


def conj_product(left_re, left_im, right_re, right_im, dc_row):
    cross_term = left_im * right_im
    real_part = left_re * right_re + jnp.where(dc_row, 0.0, cross_term)
    imag_part = jnp.where(dc_row, cross_term, left_re * right_im - left_im * right_re)
    return (real_part, imag_part)


def slab_spectrum(fwd_re, fwd_im, slab_data):
    rows = fwd_re.shape[0]
    both = jnp.dot(
        jnp.concatenate([fwd_re, fwd_im], axis=0), slab_data, preferred_element_type=jnp.float32
    ).astype(jnp.bfloat16)
    return (both[:rows], both[rows:])


def batch_spectrum(fwd_re, fwd_im, slabs):
    rows = fwd_re.shape[0]
    both = jnp.einsum(
        "fs,jsc->jfc",
        jnp.concatenate([fwd_re, fwd_im], axis=0),
        slabs,
        preferred_element_type=jnp.float32,
    ).astype(jnp.bfloat16)
    return (both[:, :rows], both[:, rows:])


def on_device(inputs, out_grad, w_in, b_in, w_mid, act_freq, w_out, decay_rate):
    tok_rows, chan_width = out_grad.shape
    fwd_re, fwd_im, inv_re, inv_im, parity, dc_row = dft_tables(tok_rows)
    parity_col = parity[:, None]
    lag_total = LAG_BLOCKS * tok_rows
    later_grads = gather_later(out_grad)
    all_lags = jnp.arange(lag_total, dtype=jnp.int32)
    filter_rows = filter_taps(all_lags, lag_total, w_in, b_in, w_mid, act_freq, w_out, decay_rate)
    spectra = [slab_spectrum(fwd_re, fwd_im, received) for received in later_grads]
    pair_list = []
    for lag_block in range(LAG_BLOCKS):
        near_re, near_im = spectra[lag_block]
        far_re, far_im = spectra[lag_block + 1]
        pair_list.append(
            (
                near_re.astype(jnp.float32) + parity_col * far_re.astype(jnp.float32),
                near_im.astype(jnp.float32) + parity_col * far_im.astype(jnp.float32),
            )
        )
    sum_re = jnp.zeros((tok_rows, chan_width), jnp.float32)
    sum_im = jnp.zeros((tok_rows, chan_width), jnp.float32)
    taps_re, taps_im = batch_spectrum(
        fwd_re, fwd_im, filter_rows.reshape(LAG_BLOCKS, tok_rows, chan_width)
    )
    for lag_block in range(LAG_BLOCKS):
        tap_re, tap_im = taps_re[lag_block], taps_im[lag_block]
        part_re, part_im = conj_product(
            tap_re.astype(jnp.float32),
            tap_im.astype(jnp.float32),
            pair_list[lag_block][0],
            pair_list[lag_block][1],
            dc_row,
        )
        sum_re = sum_re + part_re
        sum_im = sum_im + part_im
    mix_re = sum_re.astype(jnp.bfloat16)
    mix_im = sum_im.astype(jnp.bfloat16)
    inv_both = jnp.concatenate([inv_re, inv_im], axis=1)
    grad_inputs = jnp.dot(
        inv_both, jnp.concatenate([mix_re, mix_im], axis=0), preferred_element_type=jnp.float32
    ).astype(jnp.bfloat16)
    input_re, input_im = slab_spectrum(fwd_re, fwd_im, inputs)
    grad_rows = []
    for lag_block in range(LAG_BLOCKS):
        term_re, term_im = conj_product(
            input_re.astype(jnp.float32),
            input_im.astype(jnp.float32),
            pair_list[lag_block][0],
            pair_list[lag_block][1],
            dc_row,
        )
        grad_rows.append(
            jnp.dot(
                inv_both,
                jnp.concatenate([term_re, term_im], axis=0).astype(jnp.bfloat16),
                preferred_element_type=jnp.float32,
            )
        )
    row_count = lax.axis_size("row")
    share = lag_rows_total(grad_rows) // (row_count * 2)
    side_zero = lax.axis_index("side") == 0
    parts = 2 if row_count % 2 == 0 else 1
    halves = 2 if chan_width % 256 == 0 else 1
    span = chan_width // halves
    outputs = []
    gate = None
    for lane in range(halves):
        reduced = []
        for part in range(parts):
            chosen = [
                rows[:, lane * span : (lane + 1) * span]
                for rows in grad_rows[part * LAG_BLOCKS // parts : (part + 1) * LAG_BLOCKS // parts]
            ]
            staged = jnp.concatenate(chosen, axis=0).reshape(-1, 2, share, span)
            mine = jnp.where(side_zero, staged[:, 0], staged[:, 1])
            theirs = jnp.where(side_zero, staged[:, 1], staged[:, 0]).astype(jnp.bfloat16)
            if gate is not None:
                theirs, gate = lax.optimization_barrier((theirs, gate))
            received = swap_pairs(theirs, SEQ_AXES, 0, 1)
            gate = received
            reduced.append(mine + received.astype(jnp.float32))
        outputs.append(
            lax.psum_scatter(
                jnp.concatenate(reduced, axis=0).astype(jnp.bfloat16),
                "row",
                scatter_dimension=0,
                tiled=True,
            ).reshape(share, span)
        )
    grad_filter = jnp.concatenate(outputs, axis=1).astype(jnp.float32)
    return (grad_inputs, grad_filter)


def solution(mesh):
    groups, blocks, cores = mesh.devices.shape
    mesh = jax.sharding.Mesh(
        mesh.devices.reshape(groups, blocks // 2, 2, cores), ("grp", "row", "side", "ch")
    )
    placed = (
        P(("grp", "row", "side"), "ch"),
        P(("grp", "row", "side"), "ch"),
        P(),
        P(),
        P(),
        P(),
        P(None, "ch"),
        P("ch"),
    )
    return jax.shard_map(
        on_device,
        mesh=mesh,
        in_specs=placed,
        out_specs=(P(("grp", "row", "side"), "ch"), P(("grp", "row", "side"), "ch")),
        check_vma=False,
    )
```

```python
import math

import jax
import jax.numpy as jnp
from jax import lax
from jax.sharding import PartitionSpec as P

LAG_BLOCKS = 4
SEQ_AXES = ("row", "side")


def from_behind(value, axis, steps):
    count = lax.axis_size(axis)
    leading, last = (max(0, -steps), min(count, count - steps))
    return lax.ppermute(value, axis, [(source, source + steps) for source in range(leading, last)])


def swap_pairs(value, axis, from_side, stride=2):
    count = lax.axis_size(axis)
    return lax.ppermute(
        value, axis, [(source, source ^ 1) for source in range(from_side, count, stride)]
    )


def lag_rows_total(blocks):
    return sum(block.shape[0] for block in blocks)


def gather_later(block):
    side_zero = lax.axis_index(SEQ_AXES) % 2 == 0
    width = block.shape[1]
    split = width // 2 if width % 256 == 0 else width
    first_two_on = from_behind(block[:, :split], SEQ_AXES, -2)
    first_two_on, rest = lax.optimization_barrier((first_two_on, block[:, split:]))
    two_on = jnp.concatenate([first_two_on, from_behind(rest, SEQ_AXES, -2)], axis=1)
    partner_own = swap_pairs(block, SEQ_AXES, 1)
    four_on = from_behind(two_on, SEQ_AXES, -2)
    partner_two_on = jnp.concatenate(
        [swap_pairs(first_two_on, SEQ_AXES, 0, 1), swap_pairs(two_on[:, split:], SEQ_AXES, 0, 1)],
        axis=1,
    )
    partner_four_on = lax.ppermute(
        partner_two_on,
        SEQ_AXES,
        [(source, source - 2) for source in range(3, lax.axis_size(SEQ_AXES), 2)],
    )
    one_on = jnp.where(side_zero, partner_own, partner_two_on)
    three_on = jnp.where(side_zero, partner_two_on, partner_four_on)
    return [block, one_on, two_on, three_on, four_on]


def dft_tables(tok_rows):
    freq_ids = jnp.arange(tok_rows, dtype=jnp.int32)
    product = freq_ids[:, None] * freq_ids[None, :] % (2 * tok_rows)
    angles = jnp.float32(math.pi) * product.astype(jnp.float32) / tok_rows
    cosine = jnp.cos(angles)
    sine_table = jnp.sin(angles)
    parity = jnp.where(freq_ids % 2 == 0, 1.0, -1.0).astype(jnp.float32)
    dc_row = (freq_ids == 0)[:, None]
    weights = jnp.where(dc_row, 1.0, 2.0).astype(jnp.float32)
    fwd_re = cosine.astype(jnp.bfloat16)
    fwd_im = jnp.where(dc_row, parity[None, :], -sine_table).astype(jnp.bfloat16)
    inv_re = ((weights * cosine).T / (2 * tok_rows)).astype(jnp.bfloat16)
    inv_im = (jnp.where(dc_row, parity[None, :], -2.0 * sine_table).T / (2 * tok_rows)).astype(
        jnp.bfloat16
    )
    return (fwd_re, fwd_im, inv_re, inv_im, parity, dc_row)


def filter_taps(lag_ids, lag_total, w_in, b_in, w_mid, act_freq, w_out, decay_rate):
    band_count = (w_in.shape[0] - 1) // 2
    harmonic = jnp.arange(1, band_count + 1, dtype=jnp.int32)
    phases = lag_ids[:, None] * harmonic[None, :] % lag_total
    angles = 2.0 * math.pi * phases.astype(jnp.float32) / lag_total
    lag_pos = lag_ids.astype(jnp.float32)[:, None]
    features = jnp.concatenate([lag_pos / lag_total, jnp.cos(angles), jnp.sin(angles)], axis=1)
    first_act = jnp.sin(
        act_freq
        * (
            jnp.dot(
                features, w_in, precision=lax.Precision.HIGHEST, preferred_element_type=jnp.float32
            )
            + b_in
        )
    )
    second_act = jnp.sin(
        act_freq
        * jnp.dot(
            first_act, w_mid, precision=lax.Precision.HIGHEST, preferred_element_type=jnp.float32
        )
    )
    raw_taps = jnp.dot(
        second_act, w_out, precision=lax.Precision.HIGHEST, preferred_element_type=jnp.float32
    )
    return (raw_taps * jnp.exp(-decay_rate[None, :] * lag_pos)).astype(jnp.bfloat16)


def conj_product(left_re, left_im, right_re, right_im, dc_row):
    cross_term = left_im * right_im
    real_part = left_re * right_re + jnp.where(dc_row, 0.0, cross_term)
    imag_part = jnp.where(dc_row, cross_term, left_re * right_im - left_im * right_re)
    return (real_part, imag_part)


def slab_spectrum(fwd_re, fwd_im, slab_data):
    rows = fwd_re.shape[0]
    both = jnp.dot(
        jnp.concatenate([fwd_re, fwd_im], axis=0), slab_data, preferred_element_type=jnp.float32
    ).astype(jnp.bfloat16)
    return (both[:rows], both[rows:])


def batch_spectrum(fwd_re, fwd_im, slabs):
    rows = fwd_re.shape[0]
    both = jnp.einsum(
        "fs,jsc->jfc",
        jnp.concatenate([fwd_re, fwd_im], axis=0),
        slabs,
        preferred_element_type=jnp.float32,
    ).astype(jnp.bfloat16)
    return (both[:, :rows], both[:, rows:])


def on_device(inputs, out_grad, w_in, b_in, w_mid, act_freq, w_out, decay_rate):
    tok_rows, chan_width = out_grad.shape
    fwd_re, fwd_im, inv_re, inv_im, parity, dc_row = dft_tables(tok_rows)
    parity_col = parity[:, None]
    lag_total = LAG_BLOCKS * tok_rows
    later_grads = gather_later(out_grad)
    all_lags = jnp.arange(lag_total, dtype=jnp.int32)
    filter_rows = filter_taps(all_lags, lag_total, w_in, b_in, w_mid, act_freq, w_out, decay_rate)
    spectra = [slab_spectrum(fwd_re, fwd_im, received) for received in later_grads]
    pair_list = []
    for lag_block in range(LAG_BLOCKS):
        near_re, near_im = spectra[lag_block]
        far_re, far_im = spectra[lag_block + 1]
        pair_list.append(
            (
                near_re.astype(jnp.float32) + parity_col * far_re.astype(jnp.float32),
                near_im.astype(jnp.float32) + parity_col * far_im.astype(jnp.float32),
            )
        )
    sum_re = jnp.zeros((tok_rows, chan_width), jnp.float32)
    sum_im = jnp.zeros((tok_rows, chan_width), jnp.float32)
    taps_re, taps_im = batch_spectrum(
        fwd_re, fwd_im, filter_rows.reshape(LAG_BLOCKS, tok_rows, chan_width)
    )
    for lag_block in range(LAG_BLOCKS):
        tap_re, tap_im = taps_re[lag_block], taps_im[lag_block]
        part_re, part_im = conj_product(
            tap_re.astype(jnp.float32),
            tap_im.astype(jnp.float32),
            pair_list[lag_block][0],
            pair_list[lag_block][1],
            dc_row,
        )
        sum_re = sum_re + part_re
        sum_im = sum_im + part_im
    mix_re = sum_re.astype(jnp.bfloat16)
    mix_im = sum_im.astype(jnp.bfloat16)
    inv_both = jnp.concatenate([inv_re, inv_im], axis=1)
    grad_inputs = jnp.dot(
        inv_both, jnp.concatenate([mix_re, mix_im], axis=0), preferred_element_type=jnp.float32
    ).astype(jnp.bfloat16)
    input_re, input_im = slab_spectrum(fwd_re, fwd_im, inputs)
    grad_rows = []
    for lag_block in range(LAG_BLOCKS):
        term_re, term_im = conj_product(
            input_re.astype(jnp.float32),
            input_im.astype(jnp.float32),
            pair_list[lag_block][0],
            pair_list[lag_block][1],
            dc_row,
        )
        grad_rows.append(
            jnp.dot(
                inv_both,
                jnp.concatenate([term_re, term_im], axis=0).astype(jnp.bfloat16),
                preferred_element_type=jnp.float32,
            )
        )
    row_count = lax.axis_size("row")
    share = lag_rows_total(grad_rows) // (row_count * 2)
    side_zero = lax.axis_index("side") == 0
    parts = 2 if row_count % 2 == 0 else 1
    halves = 2 if chan_width % 256 == 0 else 1
    span = chan_width // halves
    outputs = []
    gate = None
    for lane in range(halves):
        reduced = []
        for part in range(parts):
            chosen = [
                rows[:, lane * span : (lane + 1) * span]
                for rows in grad_rows[part * LAG_BLOCKS // parts : (part + 1) * LAG_BLOCKS // parts]
            ]
            staged = jnp.concatenate(chosen, axis=0).reshape(-1, 2, share, span)
            mine = jnp.where(side_zero, staged[:, 0], staged[:, 1])
            theirs = jnp.where(side_zero, staged[:, 1], staged[:, 0]).astype(jnp.bfloat16)
            if gate is not None and part == 0:
                theirs, gate = lax.optimization_barrier((theirs, gate))
            received = swap_pairs(theirs, SEQ_AXES, 0, 1)
            if part == parts - 1:
                gate = received
            reduced.append(mine + received.astype(jnp.float32))
        outputs.append(
            lax.psum_scatter(
                jnp.concatenate(reduced, axis=0).astype(jnp.bfloat16),
                "row",
                scatter_dimension=0,
                tiled=True,
            ).reshape(share, span)
        )
    grad_filter = jnp.concatenate(outputs, axis=1).astype(jnp.float32)
    return (grad_inputs, grad_filter)


def solution(mesh):
    groups, blocks, cores = mesh.devices.shape
    mesh = jax.sharding.Mesh(
        mesh.devices.reshape(groups, blocks // 2, 2, cores), ("grp", "row", "side", "ch")
    )
    placed = (
        P(("grp", "row", "side"), "ch"),
        P(("grp", "row", "side"), "ch"),
        P(),
        P(),
        P(),
        P(),
        P(None, "ch"),
        P("ch"),
    )
    return jax.shard_map(
        on_device,
        mesh=mesh,
        in_specs=placed,
        out_specs=(P(("grp", "row", "side"), "ch"), P(("grp", "row", "side"), "ch")),
        check_vma=False,
    )
```

```python
import math

import jax
import jax.numpy as jnp
from jax import lax
from jax.sharding import PartitionSpec as P

LAG_BLOCKS = 4
SEQ_AXES = ("row", "side")


def from_behind(value, axis, steps):
    count = lax.axis_size(axis)
    leading, last = (max(0, -steps), min(count, count - steps))
    return lax.ppermute(value, axis, [(source, source + steps) for source in range(leading, last)])


def swap_pairs(value, axis, from_side, stride=2):
    count = lax.axis_size(axis)
    return lax.ppermute(
        value, axis, [(source, source ^ 1) for source in range(from_side, count, stride)]
    )


def lag_rows_total(blocks):
    return sum(block.shape[0] for block in blocks)


def gather_later(block):
    side_zero = lax.axis_index(SEQ_AXES) % 2 == 0
    width = block.shape[1]
    split = width // 2 if width % 256 == 0 else width
    first_two_on = from_behind(block[:, :split], SEQ_AXES, -2)
    first_two_on, rest = lax.optimization_barrier((first_two_on, block[:, split:]))
    two_on = jnp.concatenate([first_two_on, from_behind(rest, SEQ_AXES, -2)], axis=1)
    partner_own = swap_pairs(block, SEQ_AXES, 1)
    four_on = from_behind(two_on, SEQ_AXES, -2)
    partner_halves = [
        swap_pairs(first_two_on, SEQ_AXES, 0, 1),
        swap_pairs(two_on[:, split:], SEQ_AXES, 0, 1),
    ]
    partner_two_on = jnp.concatenate(partner_halves, axis=1)
    partner_four_on = jnp.concatenate(
        [
            lax.ppermute(
                piece,
                SEQ_AXES,
                [(source, source - 2) for source in range(3, lax.axis_size(SEQ_AXES), 2)],
            )
            for piece in partner_halves
        ],
        axis=1,
    )
    one_on = jnp.where(side_zero, partner_own, partner_two_on)
    three_on = jnp.where(side_zero, partner_two_on, partner_four_on)
    return [block, one_on, two_on, three_on, four_on]


def dft_tables(tok_rows):
    freq_ids = jnp.arange(tok_rows, dtype=jnp.int32)
    product = freq_ids[:, None] * freq_ids[None, :] % (2 * tok_rows)
    angles = jnp.float32(math.pi) * product.astype(jnp.float32) / tok_rows
    cosine = jnp.cos(angles)
    sine_table = jnp.sin(angles)
    parity = jnp.where(freq_ids % 2 == 0, 1.0, -1.0).astype(jnp.float32)
    dc_row = (freq_ids == 0)[:, None]
    weights = jnp.where(dc_row, 1.0, 2.0).astype(jnp.float32)
    fwd_re = cosine.astype(jnp.bfloat16)
    fwd_im = jnp.where(dc_row, parity[None, :], -sine_table).astype(jnp.bfloat16)
    inv_re = ((weights * cosine).T / (2 * tok_rows)).astype(jnp.bfloat16)
    inv_im = (jnp.where(dc_row, parity[None, :], -2.0 * sine_table).T / (2 * tok_rows)).astype(
        jnp.bfloat16
    )
    return (fwd_re, fwd_im, inv_re, inv_im, parity, dc_row)


def filter_taps(lag_ids, lag_total, w_in, b_in, w_mid, act_freq, w_out, decay_rate):
    band_count = (w_in.shape[0] - 1) // 2
    harmonic = jnp.arange(1, band_count + 1, dtype=jnp.int32)
    phases = lag_ids[:, None] * harmonic[None, :] % lag_total
    angles = 2.0 * math.pi * phases.astype(jnp.float32) / lag_total
    lag_pos = lag_ids.astype(jnp.float32)[:, None]
    features = jnp.concatenate([lag_pos / lag_total, jnp.cos(angles), jnp.sin(angles)], axis=1)
    first_act = jnp.sin(
        act_freq
        * (
            jnp.dot(
                features, w_in, precision=lax.Precision.HIGHEST, preferred_element_type=jnp.float32
            )
            + b_in
        )
    )
    second_act = jnp.sin(
        act_freq
        * jnp.dot(
            first_act, w_mid, precision=lax.Precision.HIGHEST, preferred_element_type=jnp.float32
        )
    )
    raw_taps = jnp.dot(
        second_act, w_out, precision=lax.Precision.HIGHEST, preferred_element_type=jnp.float32
    )
    return (raw_taps * jnp.exp(-decay_rate[None, :] * lag_pos)).astype(jnp.bfloat16)


def conj_product(left_re, left_im, right_re, right_im, dc_row):
    cross_term = left_im * right_im
    real_part = left_re * right_re + jnp.where(dc_row, 0.0, cross_term)
    imag_part = jnp.where(dc_row, cross_term, left_re * right_im - left_im * right_re)
    return (real_part, imag_part)


def slab_spectrum(fwd_re, fwd_im, slab_data):
    rows = fwd_re.shape[0]
    both = jnp.dot(
        jnp.concatenate([fwd_re, fwd_im], axis=0), slab_data, preferred_element_type=jnp.float32
    ).astype(jnp.bfloat16)
    return (both[:rows], both[rows:])


def batch_spectrum(fwd_re, fwd_im, slabs):
    rows = fwd_re.shape[0]
    both = jnp.einsum(
        "fs,jsc->jfc",
        jnp.concatenate([fwd_re, fwd_im], axis=0),
        slabs,
        preferred_element_type=jnp.float32,
    ).astype(jnp.bfloat16)
    return (both[:, :rows], both[:, rows:])


def on_device(inputs, out_grad, w_in, b_in, w_mid, act_freq, w_out, decay_rate):
    tok_rows, chan_width = out_grad.shape
    fwd_re, fwd_im, inv_re, inv_im, parity, dc_row = dft_tables(tok_rows)
    parity_col = parity[:, None]
    lag_total = LAG_BLOCKS * tok_rows
    later_grads = gather_later(out_grad)
    all_lags = jnp.arange(lag_total, dtype=jnp.int32)
    filter_rows = filter_taps(all_lags, lag_total, w_in, b_in, w_mid, act_freq, w_out, decay_rate)
    spectra = [slab_spectrum(fwd_re, fwd_im, received) for received in later_grads]
    pair_list = []
    for lag_block in range(LAG_BLOCKS):
        near_re, near_im = spectra[lag_block]
        far_re, far_im = spectra[lag_block + 1]
        pair_list.append(
            (
                near_re.astype(jnp.float32) + parity_col * far_re.astype(jnp.float32),
                near_im.astype(jnp.float32) + parity_col * far_im.astype(jnp.float32),
            )
        )
    sum_re = jnp.zeros((tok_rows, chan_width), jnp.float32)
    sum_im = jnp.zeros((tok_rows, chan_width), jnp.float32)
    taps_re, taps_im = batch_spectrum(
        fwd_re, fwd_im, filter_rows.reshape(LAG_BLOCKS, tok_rows, chan_width)
    )
    for lag_block in range(LAG_BLOCKS):
        tap_re, tap_im = taps_re[lag_block], taps_im[lag_block]
        part_re, part_im = conj_product(
            tap_re.astype(jnp.float32),
            tap_im.astype(jnp.float32),
            pair_list[lag_block][0],
            pair_list[lag_block][1],
            dc_row,
        )
        sum_re = sum_re + part_re
        sum_im = sum_im + part_im
    mix_re = sum_re.astype(jnp.bfloat16)
    mix_im = sum_im.astype(jnp.bfloat16)
    inv_both = jnp.concatenate([inv_re, inv_im], axis=1)
    grad_inputs = jnp.dot(
        inv_both, jnp.concatenate([mix_re, mix_im], axis=0), preferred_element_type=jnp.float32
    ).astype(jnp.bfloat16)
    input_re, input_im = slab_spectrum(fwd_re, fwd_im, inputs)
    grad_rows = []
    for lag_block in range(LAG_BLOCKS):
        term_re, term_im = conj_product(
            input_re.astype(jnp.float32),
            input_im.astype(jnp.float32),
            pair_list[lag_block][0],
            pair_list[lag_block][1],
            dc_row,
        )
        grad_rows.append(
            jnp.dot(
                inv_both,
                jnp.concatenate([term_re, term_im], axis=0).astype(jnp.bfloat16),
                preferred_element_type=jnp.float32,
            )
        )
    row_count = lax.axis_size("row")
    share = lag_rows_total(grad_rows) // (row_count * 2)
    side_zero = lax.axis_index("side") == 0
    parts = 2 if row_count % 2 == 0 else 1
    reduced = []
    for part in range(parts):
        chosen = grad_rows[part * LAG_BLOCKS // parts : (part + 1) * LAG_BLOCKS // parts]
        staged = jnp.concatenate(chosen, axis=0).reshape(-1, 2, share, chan_width)
        mine = jnp.where(side_zero, staged[:, 0], staged[:, 1])
        theirs = jnp.where(side_zero, staged[:, 1], staged[:, 0]).astype(jnp.bfloat16)
        reduced.append(mine + swap_pairs(theirs, SEQ_AXES, 0, 1).astype(jnp.float32))
    by_row = lax.psum_scatter(
        jnp.concatenate(reduced, axis=0).astype(jnp.bfloat16), "row", scatter_dimension=0, tiled=True
    )
    grad_filter = by_row.reshape(share, chan_width).astype(jnp.float32)
    return (grad_inputs, grad_filter)


def solution(mesh):
    groups, blocks, cores = mesh.devices.shape
    mesh = jax.sharding.Mesh(
        mesh.devices.reshape(groups, blocks // 2, 2, cores), ("grp", "row", "side", "ch")
    )
    placed = (
        P(("grp", "row", "side"), "ch"),
        P(("grp", "row", "side"), "ch"),
        P(),
        P(),
        P(),
        P(),
        P(None, "ch"),
        P("ch"),
    )
    return jax.shard_map(
        on_device,
        mesh=mesh,
        in_specs=placed,
        out_specs=(P(("grp", "row", "side"), "ch"), P(("grp", "row", "side"), "ch")),
        check_vma=False,
    )
```

```python
import math

import jax
import jax.numpy as jnp
from jax import lax
from jax.sharding import PartitionSpec as P

LAG_BLOCKS = 4
SEQ_AXES = ("row", "side")


def from_behind(value, axis, steps):
    count = lax.axis_size(axis)
    leading, last = (max(0, -steps), min(count, count - steps))
    return lax.ppermute(value, axis, [(source, source + steps) for source in range(leading, last)])


def swap_pairs(value, axis, from_side, stride=2):
    count = lax.axis_size(axis)
    return lax.ppermute(
        value, axis, [(source, source ^ 1) for source in range(from_side, count, stride)]
    )


def lag_rows_total(blocks):
    return sum(block.shape[0] for block in blocks)


def gather_later(block):
    side_zero = lax.axis_index(SEQ_AXES) % 2 == 0
    width = block.shape[1]
    split = width // 2 if width % 256 == 0 else width
    first_two_on = from_behind(block[:, :split], SEQ_AXES, -2)
    first_two_on, rest = lax.optimization_barrier((first_two_on, block[:, split:]))
    two_on = jnp.concatenate([first_two_on, from_behind(rest, SEQ_AXES, -2)], axis=1)
    partner_own = swap_pairs(block, SEQ_AXES, 1)
    four_on = from_behind(two_on, SEQ_AXES, -2)
    partner_two_on = jnp.concatenate(
        [swap_pairs(first_two_on, SEQ_AXES, 0, 1), swap_pairs(two_on[:, split:], SEQ_AXES, 0, 1)],
        axis=1,
    )
    partner_four_on = jnp.concatenate(
        [
            lax.ppermute(
                partner_two_on[:, :split],
                SEQ_AXES,
                [(source, source - 2) for source in range(3, lax.axis_size(SEQ_AXES), 2)],
            ),
            swap_pairs(four_on[:, split:], SEQ_AXES, 0),
        ],
        axis=1,
    )
    one_on = jnp.where(side_zero, partner_own, partner_two_on)
    three_on = jnp.where(side_zero, partner_two_on, partner_four_on)
    return [block, one_on, two_on, three_on, four_on]


def dft_tables(tok_rows):
    freq_ids = jnp.arange(tok_rows, dtype=jnp.int32)
    product = freq_ids[:, None] * freq_ids[None, :] % (2 * tok_rows)
    angles = jnp.float32(math.pi) * product.astype(jnp.float32) / tok_rows
    cosine = jnp.cos(angles)
    sine_table = jnp.sin(angles)
    parity = jnp.where(freq_ids % 2 == 0, 1.0, -1.0).astype(jnp.float32)
    dc_row = (freq_ids == 0)[:, None]
    weights = jnp.where(dc_row, 1.0, 2.0).astype(jnp.float32)
    fwd_re = cosine.astype(jnp.bfloat16)
    fwd_im = jnp.where(dc_row, parity[None, :], -sine_table).astype(jnp.bfloat16)
    inv_re = ((weights * cosine).T / (2 * tok_rows)).astype(jnp.bfloat16)
    inv_im = (jnp.where(dc_row, parity[None, :], -2.0 * sine_table).T / (2 * tok_rows)).astype(
        jnp.bfloat16
    )
    return (fwd_re, fwd_im, inv_re, inv_im, parity, dc_row)


def filter_taps(lag_ids, lag_total, w_in, b_in, w_mid, act_freq, w_out, decay_rate):
    band_count = (w_in.shape[0] - 1) // 2
    harmonic = jnp.arange(1, band_count + 1, dtype=jnp.int32)
    phases = lag_ids[:, None] * harmonic[None, :] % lag_total
    angles = 2.0 * math.pi * phases.astype(jnp.float32) / lag_total
    lag_pos = lag_ids.astype(jnp.float32)[:, None]
    features = jnp.concatenate([lag_pos / lag_total, jnp.cos(angles), jnp.sin(angles)], axis=1)
    first_act = jnp.sin(
        act_freq
        * (
            jnp.dot(
                features, w_in, precision=lax.Precision.HIGHEST, preferred_element_type=jnp.float32
            )
            + b_in
        )
    )
    second_act = jnp.sin(
        act_freq
        * jnp.dot(
            first_act, w_mid, precision=lax.Precision.HIGHEST, preferred_element_type=jnp.float32
        )
    )
    raw_taps = jnp.dot(
        second_act, w_out, precision=lax.Precision.HIGHEST, preferred_element_type=jnp.float32
    )
    return (raw_taps * jnp.exp(-decay_rate[None, :] * lag_pos)).astype(jnp.bfloat16)


def conj_product(left_re, left_im, right_re, right_im, dc_row):
    cross_term = left_im * right_im
    real_part = left_re * right_re + jnp.where(dc_row, 0.0, cross_term)
    imag_part = jnp.where(dc_row, cross_term, left_re * right_im - left_im * right_re)
    return (real_part, imag_part)


def slab_spectrum(fwd_re, fwd_im, slab_data):
    rows = fwd_re.shape[0]
    both = jnp.dot(
        jnp.concatenate([fwd_re, fwd_im], axis=0), slab_data, preferred_element_type=jnp.float32
    ).astype(jnp.bfloat16)
    return (both[:rows], both[rows:])


def batch_spectrum(fwd_re, fwd_im, slabs):
    rows = fwd_re.shape[0]
    both = jnp.einsum(
        "fs,jsc->jfc",
        jnp.concatenate([fwd_re, fwd_im], axis=0),
        slabs,
        preferred_element_type=jnp.float32,
    ).astype(jnp.bfloat16)
    return (both[:, :rows], both[:, rows:])


def on_device(inputs, out_grad, w_in, b_in, w_mid, act_freq, w_out, decay_rate):
    tok_rows, chan_width = out_grad.shape
    fwd_re, fwd_im, inv_re, inv_im, parity, dc_row = dft_tables(tok_rows)
    parity_col = parity[:, None]
    lag_total = LAG_BLOCKS * tok_rows
    later_grads = gather_later(out_grad)
    all_lags = jnp.arange(lag_total, dtype=jnp.int32)
    filter_rows = filter_taps(all_lags, lag_total, w_in, b_in, w_mid, act_freq, w_out, decay_rate)
    spectra = [slab_spectrum(fwd_re, fwd_im, received) for received in later_grads]
    pair_list = []
    for lag_block in range(LAG_BLOCKS):
        near_re, near_im = spectra[lag_block]
        far_re, far_im = spectra[lag_block + 1]
        pair_list.append(
            (
                near_re.astype(jnp.float32) + parity_col * far_re.astype(jnp.float32),
                near_im.astype(jnp.float32) + parity_col * far_im.astype(jnp.float32),
            )
        )
    sum_re = jnp.zeros((tok_rows, chan_width), jnp.float32)
    sum_im = jnp.zeros((tok_rows, chan_width), jnp.float32)
    taps_re, taps_im = batch_spectrum(
        fwd_re, fwd_im, filter_rows.reshape(LAG_BLOCKS, tok_rows, chan_width)
    )
    for lag_block in range(LAG_BLOCKS):
        tap_re, tap_im = taps_re[lag_block], taps_im[lag_block]
        part_re, part_im = conj_product(
            tap_re.astype(jnp.float32),
            tap_im.astype(jnp.float32),
            pair_list[lag_block][0],
            pair_list[lag_block][1],
            dc_row,
        )
        sum_re = sum_re + part_re
        sum_im = sum_im + part_im
    mix_re = sum_re.astype(jnp.bfloat16)
    mix_im = sum_im.astype(jnp.bfloat16)
    inv_both = jnp.concatenate([inv_re, inv_im], axis=1)
    grad_inputs = jnp.dot(
        inv_both, jnp.concatenate([mix_re, mix_im], axis=0), preferred_element_type=jnp.float32
    ).astype(jnp.bfloat16)
    input_re, input_im = slab_spectrum(fwd_re, fwd_im, inputs)
    grad_rows = []
    for lag_block in range(LAG_BLOCKS):
        term_re, term_im = conj_product(
            input_re.astype(jnp.float32),
            input_im.astype(jnp.float32),
            pair_list[lag_block][0],
            pair_list[lag_block][1],
            dc_row,
        )
        grad_rows.append(
            jnp.dot(
                inv_both,
                jnp.concatenate([term_re, term_im], axis=0).astype(jnp.bfloat16),
                preferred_element_type=jnp.float32,
            )
        )
    row_count = lax.axis_size("row")
    share = lag_rows_total(grad_rows) // (row_count * 2)
    side_zero = lax.axis_index("side") == 0
    parts = 2 if row_count % 2 == 0 else 1
    reduced = []
    for part in range(parts):
        chosen = grad_rows[part * LAG_BLOCKS // parts : (part + 1) * LAG_BLOCKS // parts]
        staged = jnp.concatenate(chosen, axis=0).reshape(-1, 2, share, chan_width)
        mine = jnp.where(side_zero, staged[:, 0], staged[:, 1])
        theirs = jnp.where(side_zero, staged[:, 1], staged[:, 0]).astype(jnp.bfloat16)
        reduced.append(mine + swap_pairs(theirs, SEQ_AXES, 0, 1).astype(jnp.float32))
    by_row = lax.psum_scatter(
        jnp.concatenate(reduced, axis=0).astype(jnp.bfloat16), "row", scatter_dimension=0, tiled=True
    )
    grad_filter = by_row.reshape(share, chan_width).astype(jnp.float32)
    return (grad_inputs, grad_filter)


def solution(mesh):
    groups, blocks, cores = mesh.devices.shape
    mesh = jax.sharding.Mesh(
        mesh.devices.reshape(groups, blocks // 2, 2, cores), ("grp", "row", "side", "ch")
    )
    placed = (
        P(("grp", "row", "side"), "ch"),
        P(("grp", "row", "side"), "ch"),
        P(),
        P(),
        P(),
        P(),
        P(None, "ch"),
        P("ch"),
    )
    return jax.shard_map(
        on_device,
        mesh=mesh,
        in_specs=placed,
        out_specs=(P(("grp", "row", "side"), "ch"), P(("grp", "row", "side"), "ch")),
        check_vma=False,
    )
```

```python
import math

import jax
import jax.numpy as jnp
from jax import lax
from jax.sharding import PartitionSpec as P

LAG_BLOCKS = 4
SEQ_AXES = ("row", "side")


def from_behind(value, axis, steps):
    count = lax.axis_size(axis)
    leading, last = (max(0, -steps), min(count, count - steps))
    return lax.ppermute(value, axis, [(source, source + steps) for source in range(leading, last)])


def swap_pairs(value, axis, from_side, stride=2):
    count = lax.axis_size(axis)
    return lax.ppermute(
        value, axis, [(source, source ^ 1) for source in range(from_side, count, stride)]
    )


def lag_rows_total(blocks):
    return sum(block.shape[0] for block in blocks)


def gather_later(block):
    side_zero = lax.axis_index(SEQ_AXES) % 2 == 0
    width = block.shape[1]
    split = width // 2 if width % 256 == 0 else width
    first_two_on = from_behind(block[:, :split], SEQ_AXES, -2)
    first_two_on, rest = lax.optimization_barrier((first_two_on, block[:, split:]))
    two_on = jnp.concatenate([first_two_on, from_behind(rest, SEQ_AXES, -2)], axis=1)
    partner_own = swap_pairs(block, SEQ_AXES, 1)
    four_on = from_behind(two_on, SEQ_AXES, -2)
    partner_two_on = jnp.concatenate(
        [swap_pairs(first_two_on, SEQ_AXES, 0, 1), swap_pairs(two_on[:, split:], SEQ_AXES, 0, 1)],
        axis=1,
    )
    partner_four_on = lax.ppermute(
        partner_two_on,
        SEQ_AXES,
        [(source, source - 2) for source in range(3, lax.axis_size(SEQ_AXES), 2)],
    )
    one_on = jnp.where(side_zero, partner_own, partner_two_on)
    three_on = jnp.where(side_zero, partner_two_on, partner_four_on)
    return [block, one_on, two_on, three_on, four_on]


def dft_tables(tok_rows):
    freq_ids = jnp.arange(tok_rows, dtype=jnp.int32)
    product = freq_ids[:, None] * freq_ids[None, :] % (2 * tok_rows)
    angles = jnp.float32(math.pi) * product.astype(jnp.float32) / tok_rows
    cosine = jnp.cos(angles)
    sine_table = jnp.sin(angles)
    parity = jnp.where(freq_ids % 2 == 0, 1.0, -1.0).astype(jnp.float32)
    dc_row = (freq_ids == 0)[:, None]
    weights = jnp.where(dc_row, 1.0, 2.0).astype(jnp.float32)
    fwd_re = cosine.astype(jnp.bfloat16)
    fwd_im = jnp.where(dc_row, parity[None, :], -sine_table).astype(jnp.bfloat16)
    inv_re = ((weights * cosine).T / (2 * tok_rows)).astype(jnp.bfloat16)
    inv_im = (jnp.where(dc_row, parity[None, :], -2.0 * sine_table).T / (2 * tok_rows)).astype(
        jnp.bfloat16
    )
    return (fwd_re, fwd_im, inv_re, inv_im, parity, dc_row)


def filter_taps(lag_ids, lag_total, w_in, b_in, w_mid, act_freq, w_out, decay_rate):
    band_count = (w_in.shape[0] - 1) // 2
    harmonic = jnp.arange(1, band_count + 1, dtype=jnp.int32)
    phases = lag_ids[:, None] * harmonic[None, :] % lag_total
    angles = 2.0 * math.pi * phases.astype(jnp.float32) / lag_total
    lag_pos = lag_ids.astype(jnp.float32)[:, None]
    features = jnp.concatenate([lag_pos / lag_total, jnp.cos(angles), jnp.sin(angles)], axis=1)
    first_act = jnp.sin(
        act_freq
        * (
            jnp.dot(
                features, w_in, precision=lax.Precision.HIGHEST, preferred_element_type=jnp.float32
            )
            + b_in
        )
    )
    second_act = jnp.sin(
        act_freq
        * jnp.dot(
            first_act, w_mid, precision=lax.Precision.HIGHEST, preferred_element_type=jnp.float32
        )
    )
    raw_taps = jnp.dot(
        second_act, w_out, precision=lax.Precision.HIGHEST, preferred_element_type=jnp.float32
    )
    return (raw_taps * jnp.exp(-decay_rate[None, :] * lag_pos)).astype(jnp.bfloat16)


def conj_product(left_re, left_im, right_re, right_im, dc_row):
    cross_term = left_im * right_im
    real_part = left_re * right_re + jnp.where(dc_row, 0.0, cross_term)
    imag_part = jnp.where(dc_row, cross_term, left_re * right_im - left_im * right_re)
    return (real_part, imag_part)


def slab_spectrum(fwd_re, fwd_im, slab_data):
    rows = fwd_re.shape[0]
    both = jnp.dot(
        jnp.concatenate([fwd_re, fwd_im], axis=0), slab_data, preferred_element_type=jnp.float32
    ).astype(jnp.bfloat16)
    return (both[:rows], both[rows:])


def batch_spectrum(fwd_re, fwd_im, slabs):
    rows = fwd_re.shape[0]
    both = jnp.einsum(
        "fs,jsc->jfc",
        jnp.concatenate([fwd_re, fwd_im], axis=0),
        slabs,
        preferred_element_type=jnp.float32,
    ).astype(jnp.bfloat16)
    return (both[:, :rows], both[:, rows:])


def on_device(inputs, out_grad, w_in, b_in, w_mid, act_freq, w_out, decay_rate):
    tok_rows, chan_width = out_grad.shape
    fwd_re, fwd_im, inv_re, inv_im, parity, dc_row = dft_tables(tok_rows)
    parity_col = parity[:, None]
    lag_total = LAG_BLOCKS * tok_rows
    later_grads = gather_later(out_grad)
    all_lags = jnp.arange(lag_total, dtype=jnp.int32)
    filter_rows = filter_taps(all_lags, lag_total, w_in, b_in, w_mid, act_freq, w_out, decay_rate)
    spectra = [slab_spectrum(fwd_re, fwd_im, received) for received in later_grads]
    pair_list = []
    for lag_block in range(LAG_BLOCKS):
        near_re, near_im = spectra[lag_block]
        far_re, far_im = spectra[lag_block + 1]
        pair_list.append(
            (
                near_re.astype(jnp.float32) + parity_col * far_re.astype(jnp.float32),
                near_im.astype(jnp.float32) + parity_col * far_im.astype(jnp.float32),
            )
        )
    sum_re = jnp.zeros((tok_rows, chan_width), jnp.float32)
    sum_im = jnp.zeros((tok_rows, chan_width), jnp.float32)
    taps_re, taps_im = batch_spectrum(
        fwd_re, fwd_im, filter_rows.reshape(LAG_BLOCKS, tok_rows, chan_width)
    )
    for lag_block in range(LAG_BLOCKS):
        tap_re, tap_im = taps_re[lag_block], taps_im[lag_block]
        part_re, part_im = conj_product(
            tap_re.astype(jnp.float32),
            tap_im.astype(jnp.float32),
            pair_list[lag_block][0],
            pair_list[lag_block][1],
            dc_row,
        )
        sum_re = sum_re + part_re
        sum_im = sum_im + part_im
    mix_re = sum_re.astype(jnp.bfloat16)
    mix_im = sum_im.astype(jnp.bfloat16)
    inv_both = jnp.concatenate([inv_re, inv_im], axis=1)
    grad_inputs = jnp.dot(
        inv_both, jnp.concatenate([mix_re, mix_im], axis=0), preferred_element_type=jnp.float32
    ).astype(jnp.bfloat16)
    input_re, input_im = slab_spectrum(fwd_re, fwd_im, inputs)
    row_count = lax.axis_size("row")
    share = LAG_BLOCKS * tok_rows // (row_count * 2)
    side_zero = lax.axis_index("side") == 0
    inv_sides = inv_both.reshape(-1, 2, share, inv_both.shape[1])
    inv_mine = jnp.where(side_zero, inv_sides[:, 0], inv_sides[:, 1]).reshape(-1, inv_both.shape[1])
    inv_theirs = jnp.where(side_zero, inv_sides[:, 1], inv_sides[:, 0]).reshape(
        -1, inv_both.shape[1]
    )
    mine_rows = []
    theirs_rows = []
    for lag_block in range(LAG_BLOCKS):
        term_re, term_im = conj_product(
            input_re.astype(jnp.float32),
            input_im.astype(jnp.float32),
            pair_list[lag_block][0],
            pair_list[lag_block][1],
            dc_row,
        )
        stacked = jnp.concatenate([term_re, term_im], axis=0).astype(jnp.bfloat16)
        theirs_rows.append(
            jnp.dot(inv_theirs, stacked, preferred_element_type=jnp.float32).astype(jnp.bfloat16)
        )
        mine_rows.append(jnp.dot(inv_mine, stacked, preferred_element_type=jnp.float32))
    parts = 2 if row_count % 2 == 0 else 1
    reduced = []
    for part in range(parts):
        low, high = part * LAG_BLOCKS // parts, (part + 1) * LAG_BLOCKS // parts
        mine = jnp.concatenate(mine_rows[low:high], axis=0).reshape(-1, share, chan_width)
        theirs = jnp.concatenate(theirs_rows[low:high], axis=0).reshape(-1, share, chan_width)
        reduced.append(mine + swap_pairs(theirs, SEQ_AXES, 0, 1).astype(jnp.float32))
    by_row = lax.psum_scatter(
        jnp.concatenate(reduced, axis=0).astype(jnp.bfloat16), "row", scatter_dimension=0, tiled=True
    )
    grad_filter = by_row.reshape(share, chan_width).astype(jnp.float32)
    return (grad_inputs, grad_filter)


def solution(mesh):
    groups, blocks, cores = mesh.devices.shape
    mesh = jax.sharding.Mesh(
        mesh.devices.reshape(groups, blocks // 2, 2, cores), ("grp", "row", "side", "ch")
    )
    placed = (
        P(("grp", "row", "side"), "ch"),
        P(("grp", "row", "side"), "ch"),
        P(),
        P(),
        P(),
        P(),
        P(None, "ch"),
        P("ch"),
    )
    return jax.shard_map(
        on_device,
        mesh=mesh,
        in_specs=placed,
        out_specs=(P(("grp", "row", "side"), "ch"), P(("grp", "row", "side"), "ch")),
        check_vma=False,
    )
```

```python
import math

import jax
import jax.numpy as jnp
from jax import lax
from jax.sharding import PartitionSpec as P

LAG_BLOCKS = 4
SEQ_AXES = ("row", "side")


def from_behind(value, axis, steps):
    count = lax.axis_size(axis)
    leading, last = (max(0, -steps), min(count, count - steps))
    return lax.ppermute(value, axis, [(source, source + steps) for source in range(leading, last)])


def swap_pairs(value, axis, from_side, stride=2):
    count = lax.axis_size(axis)
    return lax.ppermute(
        value, axis, [(source, source ^ 1) for source in range(from_side, count, stride)]
    )


def lag_rows_total(blocks):
    return sum(block.shape[0] for block in blocks)


def gather_later(block):
    side_zero = lax.axis_index(SEQ_AXES) % 2 == 0
    width = block.shape[1]
    split = width // 2 if width % 256 == 0 else width
    first_two_on = from_behind(block[:, :split], SEQ_AXES, -2)
    first_two_on, rest = lax.optimization_barrier((first_two_on, block[:, split:]))
    two_on = jnp.concatenate([first_two_on, from_behind(rest, SEQ_AXES, -2)], axis=1)
    partner_own = swap_pairs(block, SEQ_AXES, 1)
    four_on = from_behind(two_on, SEQ_AXES, -2)
    partner_two_on = jnp.concatenate(
        [swap_pairs(first_two_on, SEQ_AXES, 0, 1), swap_pairs(two_on[:, split:], SEQ_AXES, 0, 1)],
        axis=1,
    )
    partner_four_on = lax.ppermute(
        partner_two_on,
        SEQ_AXES,
        [(source, source - 2) for source in range(3, lax.axis_size(SEQ_AXES), 2)],
    )
    one_on = jnp.where(side_zero, partner_own, partner_two_on)
    three_on = jnp.where(side_zero, partner_two_on, partner_four_on)
    return [block, one_on, two_on, three_on, four_on]


def dft_tables(tok_rows):
    freq_ids = jnp.arange(tok_rows, dtype=jnp.int32)
    product = freq_ids[:, None] * freq_ids[None, :] % (2 * tok_rows)
    angles = jnp.float32(math.pi) * product.astype(jnp.float32) / tok_rows
    cosine = jnp.cos(angles)
    sine_table = jnp.sin(angles)
    parity = jnp.where(freq_ids % 2 == 0, 1.0, -1.0).astype(jnp.float32)
    dc_row = (freq_ids == 0)[:, None]
    weights = jnp.where(dc_row, 1.0, 2.0).astype(jnp.float32)
    fwd_re = cosine.astype(jnp.bfloat16)
    fwd_im = jnp.where(dc_row, parity[None, :], -sine_table).astype(jnp.bfloat16)
    inv_re = ((weights * cosine).T / (2 * tok_rows)).astype(jnp.bfloat16)
    inv_im = (jnp.where(dc_row, parity[None, :], -2.0 * sine_table).T / (2 * tok_rows)).astype(
        jnp.bfloat16
    )
    return (fwd_re, fwd_im, inv_re, inv_im, parity, dc_row)


def filter_taps(lag_ids, lag_total, w_in, b_in, w_mid, act_freq, w_out, decay_rate):
    band_count = (w_in.shape[0] - 1) // 2
    harmonic = jnp.arange(1, band_count + 1, dtype=jnp.int32)
    phases = lag_ids[:, None] * harmonic[None, :] % lag_total
    angles = 2.0 * math.pi * phases.astype(jnp.float32) / lag_total
    lag_pos = lag_ids.astype(jnp.float32)[:, None]
    features = jnp.concatenate([lag_pos / lag_total, jnp.cos(angles), jnp.sin(angles)], axis=1)
    first_act = jnp.sin(
        act_freq
        * (
            jnp.dot(
                features, w_in, precision=lax.Precision.HIGHEST, preferred_element_type=jnp.float32
            )
            + b_in
        )
    )
    second_act = jnp.sin(
        act_freq
        * jnp.dot(
            first_act, w_mid, precision=lax.Precision.HIGHEST, preferred_element_type=jnp.float32
        )
    )
    raw_taps = jnp.dot(
        second_act, w_out, precision=lax.Precision.HIGHEST, preferred_element_type=jnp.float32
    )
    return (raw_taps * jnp.exp(-decay_rate[None, :] * lag_pos)).astype(jnp.bfloat16)


def conj_product(left_re, left_im, right_re, right_im, dc_row):
    cross_term = left_im * right_im
    real_part = left_re * right_re + jnp.where(dc_row, 0.0, cross_term)
    imag_part = jnp.where(dc_row, cross_term, left_re * right_im - left_im * right_re)
    return (real_part, imag_part)


def slab_spectrum(fwd_re, fwd_im, slab_data):
    rows = fwd_re.shape[0]
    both = jnp.dot(
        jnp.concatenate([fwd_re, fwd_im], axis=0), slab_data, preferred_element_type=jnp.float32
    ).astype(jnp.bfloat16)
    return (both[:rows], both[rows:])


def batch_spectrum(fwd_re, fwd_im, slabs):
    rows = fwd_re.shape[0]
    both = jnp.einsum(
        "fs,jsc->jfc",
        jnp.concatenate([fwd_re, fwd_im], axis=0),
        slabs,
        preferred_element_type=jnp.float32,
    ).astype(jnp.bfloat16)
    return (both[:, :rows], both[:, rows:])


def on_device(inputs, out_grad, w_in, b_in, w_mid, act_freq, w_out, decay_rate):
    tok_rows, chan_width = out_grad.shape
    fwd_re, fwd_im, inv_re, inv_im, parity, dc_row = dft_tables(tok_rows)
    parity_col = parity[:, None]
    lag_total = LAG_BLOCKS * tok_rows
    later_grads = gather_later(out_grad)
    all_lags = jnp.arange(lag_total, dtype=jnp.int32)
    filter_rows = filter_taps(all_lags, lag_total, w_in, b_in, w_mid, act_freq, w_out, decay_rate)
    spectra = [slab_spectrum(fwd_re, fwd_im, received) for received in later_grads]
    pair_list = []
    for lag_block in range(LAG_BLOCKS):
        near_re, near_im = spectra[lag_block]
        far_re, far_im = spectra[lag_block + 1]
        pair_list.append(
            (
                near_re.astype(jnp.float32) + parity_col * far_re.astype(jnp.float32),
                near_im.astype(jnp.float32) + parity_col * far_im.astype(jnp.float32),
            )
        )
    sum_re = jnp.zeros((tok_rows, chan_width), jnp.float32)
    sum_im = jnp.zeros((tok_rows, chan_width), jnp.float32)
    taps_re, taps_im = batch_spectrum(
        fwd_re, fwd_im, filter_rows.reshape(LAG_BLOCKS, tok_rows, chan_width)
    )
    for lag_block in range(LAG_BLOCKS):
        tap_re, tap_im = taps_re[lag_block], taps_im[lag_block]
        part_re, part_im = conj_product(
            tap_re.astype(jnp.float32),
            tap_im.astype(jnp.float32),
            pair_list[lag_block][0],
            pair_list[lag_block][1],
            dc_row,
        )
        sum_re = sum_re + part_re
        sum_im = sum_im + part_im
    mix_re = sum_re.astype(jnp.bfloat16)
    mix_im = sum_im.astype(jnp.bfloat16)
    inv_both = jnp.concatenate([inv_re, inv_im], axis=1)
    grad_inputs = jnp.dot(
        inv_both, jnp.concatenate([mix_re, mix_im], axis=0), preferred_element_type=jnp.float32
    ).astype(jnp.bfloat16)
    input_re, input_im = slab_spectrum(fwd_re, fwd_im, inputs)
    row_count = lax.axis_size("row")
    share = LAG_BLOCKS * tok_rows // (row_count * 2)
    side_zero = lax.axis_index("side") == 0
    inv_sides = inv_both.reshape(-1, 2, share, inv_both.shape[1])
    inv_mine = jnp.where(side_zero, inv_sides[:, 0], inv_sides[:, 1]).reshape(-1, inv_both.shape[1])
    inv_theirs = jnp.where(side_zero, inv_sides[:, 1], inv_sides[:, 0]).reshape(
        -1, inv_both.shape[1]
    )
    mine_rows = []
    for lag_block in range(LAG_BLOCKS):
        term_re, term_im = conj_product(
            input_re.astype(jnp.float32),
            input_im.astype(jnp.float32),
            pair_list[lag_block][0],
            pair_list[lag_block][1],
            dc_row,
        )
        mine_rows.append(jnp.concatenate([term_re, term_im], axis=0).astype(jnp.bfloat16))
    parts = 2 if row_count % 2 == 0 else 1
    reduced = []
    for part in range(parts):
        low, high = part * LAG_BLOCKS // parts, (part + 1) * LAG_BLOCKS // parts
        stacked = jnp.stack(mine_rows[low:high], axis=0)
        theirs = jnp.einsum(
            "rk,jkc->jrc", inv_theirs, stacked, preferred_element_type=jnp.float32
        ).astype(jnp.bfloat16).reshape(-1, share, chan_width)
        mine = jnp.einsum(
            "rk,jkc->jrc", inv_mine, stacked, preferred_element_type=jnp.float32
        ).reshape(-1, share, chan_width)
        reduced.append(mine + swap_pairs(theirs, SEQ_AXES, 0, 1).astype(jnp.float32))
    by_row = lax.psum_scatter(
        jnp.concatenate(reduced, axis=0).astype(jnp.bfloat16), "row", scatter_dimension=0, tiled=True
    )
    grad_filter = by_row.reshape(share, chan_width).astype(jnp.float32)
    return (grad_inputs, grad_filter)


def solution(mesh):
    groups, blocks, cores = mesh.devices.shape
    mesh = jax.sharding.Mesh(
        mesh.devices.reshape(groups, blocks // 2, 2, cores), ("grp", "row", "side", "ch")
    )
    placed = (
        P(("grp", "row", "side"), "ch"),
        P(("grp", "row", "side"), "ch"),
        P(),
        P(),
        P(),
        P(),
        P(None, "ch"),
        P("ch"),
    )
    return jax.shard_map(
        on_device,
        mesh=mesh,
        in_specs=placed,
        out_specs=(P(("grp", "row", "side"), "ch"), P(("grp", "row", "side"), "ch")),
        check_vma=False,
    )
```
